256 devices in a mesh: tok: 64 (over y, z, core), head: 4 (over x).
Axes of the slice: x: 4, y: 4, z: 8, core: 2. Of those that a mesh axis runs over, the one named last changes fastest.
Arguments:
- hidden: bfloat16 [2048, 2048], P('tok', 'head'), may hold values from -24 to 24
- attn_gain: float32 [2048], replicated, may hold values from 0.1 to 1.9
- w_query: bfloat16 [2048, 3072], P(None, 'head'), may hold values from -0.125 to 0.125
- w_latent: bfloat16 [2048, 576], P('head'), may hold values from -0.125 to 0.125
- w_key_up: bfloat16 [16, 128, 512], P('head'), may hold values from -0.5 to 0.5
- w_value_up: bfloat16 [16, 512, 128], P('head'), may hold values from -1 to 1
- w_out: bfloat16 [2048, 2048], P('head'), may hold values from -0.125 to 0.125
- latent_cache: bfloat16 [638976, 576], P(('tok', 'head')), may hold values from -6 to 6
- cache_lengths: int32 [2048], P('tok'), may hold values from 144 to 2048, as said below
- request_slot: int32 [2048], P('tok'), may hold values from 0 to 2047, as said below
- ffn_gain: float32 [2048], P('head'), may hold values from 0.1 to 1.9
- w_router: bfloat16 [2048, 64], P('head'), may hold values from -0.25 to 0.25
- routes: int32 [2048, 6], P('tok'), may hold values from 0 to 63, all different within a row; in each aligned block of 32 rows (0 to 31, 32 to 63, ...) at most 6 rows name the same one
- expert_gate: bfloat16 [64, 2048, 1408], P('tok', None, 'head'), may hold values from -0.125 to 0.125
- expert_up: bfloat16 [64, 2048, 1408], P('tok', None, 'head'), may hold values from -0.125 to 0.125
- expert_down: bfloat16 [64, 1408, 2048], P('tok', 'head'), may hold values from -0.15625 to 0.15625
Outputs:
- new_entry: bfloat16 [2048, 576], P('tok')
- attended: bfloat16 [2048, 2048], P('tok', 'head')
- expert_mix: bfloat16 [2048, 2048], P('tok', 'head')
The draws below stay inside these ranges and needn't reach their ends.
Inputs may be any that keep to these rules, and one draw needn't show every extreme that they name: `request_slot`: a permutation of the 2048 slots; slot s lies on owner s // 32, so every owner holds 32 slots; the requests of one device name at most 1 slots of one owner, and every device reaches that bound. `cache_lengths`: the caches of an owner's slots lie end to end in slot order at the start of that owner's 9984 rows of latent_cache; they fill at most 9984 rows, and some owner fills all of them. `routes`: each row names 6 different experts; in the rows of one device no expert is named more than 6 times.
All inputs are finite; a program needn't handle non-finite values.
Results may differ from the reference program's by a relative error of at most 0.028.
Values may be sent and summed in bfloat16 or wider, within the bound.
No kernel may reach another device: no remote copies, remote signals or barrier semaphores. Data moves between devices by JAX's collectives and lax.ppermute only.
A program may use at most 128 MiB of HBM per device.

```python
import math
import jax
import jax.numpy as jnp
import numpy as np
from jax import lax

D = 2048
HEADS = 16
NOPE = 128
ROPE = 64
LATENT = 512
FF = 1408
TOPK = 6
REQ_DEV = 32
LONG_LEN = 2048
SHORT_MOST = 256
SHORT_LEAST = 144
EXPERTS = 64
REQUESTS = 2048
CACHE_DEV = 9984
ROUTE_MOST = 6
N_TOK = 64


def shuffled(subkey):
    return jax.random.permutation(subkey, REQ_DEV)


def slot_plan(key):
    folded = jax.random.fold_in(key, 7)
    subkeys = jax.random.split(folded, 9)
    owners_count = REQUESTS // REQ_DEV
    member = jnp.arange(REQ_DEV, dtype=jnp.int32)
    shifts = jax.random.permutation(subkeys[0], owners_count).astype(jnp.int32)
    offsets = shifts[member % owners_count]
    layout = jax.random.permutation(subkeys[1], owners_count).astype(jnp.int32)
    order_in = jax.vmap(shuffled)(jax.random.split(subkeys[2], owners_count)).astype(jnp.int32)
    within = jax.vmap(shuffled)(jax.random.split(subkeys[3], owners_count)).astype(jnp.int32)
    senders = jnp.arange(owners_count, dtype=jnp.int32)[:, None]
    target = layout[(senders + offsets[order_in]) % owners_count]
    slot_index = within[target, order_in]
    request_slot = (target * REQ_DEV + slot_index).reshape(-1).astype(jnp.int32)
    owner_ids = jnp.arange(owners_count, dtype=jnp.int32)
    shorts = jax.random.randint(subkeys[4], (owners_count, REQ_DEV), SHORT_LEAST, SHORT_MOST + 1, dtype=jnp.int32)
    fullest = jax.random.randint(subkeys[5], (), 0, owners_count, dtype=jnp.int32)
    chosen = (jax.random.randint(subkeys[6], (owners_count,), 0, 2, dtype=jnp.int32) == 1) | (owner_ids == fullest)
    long_at = jax.random.randint(subkeys[7], (owners_count,), 0, REQ_DEV, dtype=jnp.int32)
    long_size = jax.random.randint(subkeys[8], (owners_count,), LONG_LEN - LONG_LEN // 8, LONG_LEN + 1, dtype=jnp.int32)
    long_size = jnp.where(owner_ids == fullest, LONG_LEN, long_size)
    shorts = jnp.where((owner_ids == fullest)[:, None], SHORT_MOST, shorts)
    is_long = chosen[:, None] & (member[None, :] == long_at[:, None])
    by_slot = jnp.where(is_long, long_size[:, None], shorts).reshape(-1).astype(jnp.int32)
    cache_lengths = by_slot[request_slot]
    return (request_slot, cache_lengths)


def draw_request_slot(key, part):
    return slot_plan(key)[0]


def draw_cache_lengths(key, part):
    return slot_plan(key)[1]


def draw_hidden(key, part):
    subkeys = jax.random.split(key, 3)
    columns = jnp.arange(D, dtype=jnp.float32)
    col_scale = 0.6 * 3.0 ** (0.5 * columns / D) * jnp.exp(jax.random.uniform(subkeys[1], (D,), jnp.float32, -0.3, 0.3))
    row_scale = jnp.exp(jax.random.uniform(subkeys[2], (REQUESTS, 1), jnp.float32, -0.4, 0.4))
    sample = jnp.clip(jax.random.normal(subkeys[0], (REQUESTS, D), jnp.float32), -6.0, 6.0)
    return jnp.clip(sample * row_scale * col_scale[None, :], -24.0, 24.0).astype(jnp.bfloat16)


def level_of(key, shape, cuts, least, high):
    gain, own = 1.0, jax.random.fold_in(key, 6)
    for dim, parts in cuts:
        heights = jnp.exp(jax.random.uniform(jax.random.fold_in(own, dim), (parts,), jnp.float32, least / len(cuts), high / len(cuts)))
        gain = gain * jnp.repeat(heights, shape[dim] // parts).reshape([-1 if axis == dim else 1 for axis in range(len(shape))])
    return gain


def shared_out(key, own, number, rows, count, top, limit, skew):
    sequence = jax.random.permutation(key, count)
    packed, ordinary = shares(count, rows * top, limit, skew, True), shares(count, rows * top, limit, skew, False)
    places = jnp.arange(count)

    def named(lengths, rotation):
        used = int((lengths > 0).sum())
        fixed = max(1, used // 4)
        passed = fixed + (places - fixed + rotation * (used - fixed)) % max(1, count - fixed)
        return jnp.zeros((count,), jnp.int32).at[sequence[jnp.where(places < fixed, places, passed)]].set(jnp.asarray(lengths, jnp.int32))

    lengths = jnp.where(number % 4 == 0, named(packed, number // 4), named(ordinary, number - number // 4 - 1))
    mixed = jax.random.permutation(jax.random.fold_in(own, 3), count)
    giver, sink = mixed[0:count // 2 * 2:2], mixed[1:count // 2 * 2:2]
    margin = jnp.minimum(lengths[giver] - 1, limit - lengths[sink]) // 2
    margin = jnp.where((giver == sequence[0]) | (sink == sequence[0]) | (lengths[sink] == 0), 0, jnp.maximum(margin, 0))
    passed = jax.random.randint(jax.random.fold_in(own, 4), (count // 2,), 0, 1 << 20) % (margin + 1)
    lengths = lengths.at[giver].add(-passed).at[sink].add(passed)
    members = jnp.searchsorted(jnp.cumsum(lengths), jnp.arange(rows * top), side="right").astype(jnp.int32)
    grid = members.reshape(top, rows).T
    grid = grid[jax.random.permutation(jax.random.fold_in(own, 1), rows)]
    rotation = jax.random.randint(jax.random.fold_in(own, 2), (rows, 1), 0, top)
    return jnp.take_along_axis(grid, (jnp.arange(top)[None, :] + rotation) % top, axis=1)


def shares(amount, total, reach, lean, full):
    loads = [(1 << 20) // math.isqrt(rank ** lean) + 1 for rank in range(1, amount + 1)]
    largest = reach if full else min(reach, max(-(-total // amount), total * loads[0] // sum(loads)))
    least = 1 if total - largest >= amount - 1 else 0
    counts, spare = [largest] + [least] * (amount - 1), total - largest - least * (amount - 1)
    while spare > 0:
        candidates = [i for i in range(1, amount) if counts[i] < largest] or [i for i in range(1, amount) if counts[i] < reach]
        whole, budget = sum([loads[i] for i in candidates]), spare
        for i in candidates:
            addition = min(reach - counts[i], max(1, budget * loads[i] // whole), spare)
            counts[i] = counts[i] + addition
            spare = spare - addition
    return np.array(counts)


def bell_draw(rng, dims, scale, reach, cuts=(), kind=jnp.bfloat16):
    array = jax.random.normal(rng, dims, jnp.float32) * scale
    if len(cuts) > 0:
        array = level_of(rng, dims, cuts, -0.22, 0.18) * array
    return jnp.clip(array, min=-reach, max=reach).astype(kind)


def setup_inputs(seed: int = 0) -> dict:
    arg_keys = jax.random.split(jax.random.key(seed), 17)
    hidden = draw_hidden(jax.random.fold_in(arg_keys[16], 71), 0)
    attn_gain = jnp.clip(1.0 + 0.18 * jax.random.normal(arg_keys[1], (D,), jnp.float32), 0.1, 1.9)
    w_query = bell_draw(arg_keys[2], (D, HEADS * (NOPE + ROPE)), D ** -0.5, 0.125, ((1, 4),))
    w_latent = bell_draw(arg_keys[3], (D, LATENT + ROPE), D ** -0.5, 0.125, ((0, 4),))
    w_key_up = bell_draw(arg_keys[4], (HEADS, NOPE, LATENT), NOPE ** -0.5, 0.5, ((0, 4),))
    w_value_up = bell_draw(arg_keys[5], (HEADS, LATENT, NOPE), (LATENT // 16) ** -0.5, 1.0, ((0, 4),))
    w_out = bell_draw(arg_keys[6], (HEADS * NOPE, D), (HEADS * NOPE) ** -0.5, 0.125, ((0, 4),))
    latent_cache = bell_draw(arg_keys[7], (N_TOK * CACHE_DEV, LATENT + ROPE), 1.0, 6.0, ((0, 256),))
    cache_lengths = draw_cache_lengths(jax.random.fold_in(arg_keys[16], 71), 0)
    request_slot = draw_request_slot(jax.random.fold_in(arg_keys[16], 71), 0)
    ffn_gain = jnp.clip(1.0 + 0.18 * jax.random.normal(arg_keys[10], (D,), jnp.float32), 0.1, 1.9)
    w_router = bell_draw(arg_keys[11], (D, EXPERTS), (D // 4) ** -0.5, 0.25, ((0, 4),))
    routes_keys = jax.random.split(jax.random.fold_in(arg_keys[12], 1), REQUESTS // REQ_DEV)
    routes_turns = jax.random.permutation(jax.random.fold_in(arg_keys[12], 3), REQUESTS // REQ_DEV)
    routes = jax.vmap(lambda own, number: shared_out(jax.random.fold_in(arg_keys[12], 2), own, number, REQ_DEV, EXPERTS, TOPK, ROUTE_MOST, 2))(routes_keys, routes_turns).reshape((REQUESTS, TOPK))
    expert_gate = bell_draw(arg_keys[13], (EXPERTS, D, FF), D ** -0.5, 0.125, ((0, 64), (2, 4)))
    expert_up = bell_draw(arg_keys[14], (EXPERTS, D, FF), D ** -0.5, 0.125, ((0, 64), (2, 4)))
    expert_down = bell_draw(arg_keys[15], (EXPERTS, FF, D), FF ** -0.5, 0.15625, ((0, 64), (1, 4)))
    return dict(hidden=hidden, attn_gain=attn_gain, w_query=w_query, w_latent=w_latent, w_key_up=w_key_up, w_value_up=w_value_up, w_out=w_out, latent_cache=latent_cache, cache_lengths=cache_lengths, request_slot=request_slot, ffn_gain=ffn_gain, w_router=w_router, routes=routes, expert_gate=expert_gate, expert_up=expert_up, expert_down=expert_down)


NORM_EPS = 1e-06

def rotate_pairs(values, places):
    halfway = values.shape[-1] // 2
    freqs = 10000.0 ** (-jnp.arange(halfway, dtype=jnp.float32) / halfway)
    angles = places.astype(jnp.float32).reshape(places.shape + (1,) * (values.ndim - 1)) * freqs
    cosine = jnp.cos(angles)
    sine = jnp.sin(angles)
    first_half = values[..., :halfway]
    second_half = values[..., halfway:]
    return jnp.concatenate([first_half * cosine - second_half * sine, first_half * sine + second_half * cosine], axis=-1)

def owner_attention(bundle):
    slot_probes, owner_rows, slot_lengths = bundle
    starts = jnp.cumsum(slot_lengths) - slot_lengths
    places = jnp.arange(owner_rows.shape[0], dtype=jnp.int32)
    inside = (places[None, :] >= starts[:, None]) & (places[None, :] < (starts + slot_lengths)[:, None])
    factor = (NOPE + ROPE) ** (-0.5)
    scores = factor * jnp.einsum('khc,pc->khp', slot_probes.astype(jnp.float32), owner_rows.astype(jnp.float32), precision=lax.Precision.HIGHEST)
    weights = jnp.where(inside[:, None, :], jnp.exp(scores), 0.0).astype(jnp.bfloat16)
    numerator = jnp.einsum('khp,pl->khl', weights.astype(jnp.float32), owner_rows[:, :LATENT].astype(jnp.float32), precision=lax.Precision.HIGHEST)
    denominator = lax.optimization_barrier(jnp.sum(weights.astype(jnp.float32), axis=2))
    return (numerator, denominator)

def reference(hidden, attn_gain, w_query, w_latent, w_key_up, w_value_up, w_out, latent_cache, cache_lengths, request_slot, ffn_gain, w_router, routes, expert_gate, expert_up, expert_down):
    owners_count = REQUESTS // REQ_DEV
    wide_hidden = hidden.astype(jnp.float32)
    inv_attn = lax.rsqrt(lax.optimization_barrier(jnp.mean(wide_hidden * wide_hidden, axis=1, keepdims=True)) + NORM_EPS)
    normed_attn = (wide_hidden * inv_attn * attn_gain).astype(jnp.bfloat16)
    queries = jnp.dot(normed_attn, w_query, preferred_element_type=jnp.float32).astype(jnp.bfloat16)
    queries = queries.reshape(REQUESTS, HEADS, NOPE + ROPE)
    compressed = jnp.dot(normed_attn, w_latent, preferred_element_type=jnp.float32)
    latent_new = compressed[:, :LATENT]
    latent_new = latent_new * lax.rsqrt(lax.optimization_barrier(jnp.mean(latent_new * latent_new, axis=1, keepdims=True)) + NORM_EPS)
    new_entry = jnp.concatenate([latent_new, rotate_pairs(compressed[:, LATENT:], cache_lengths)], axis=1).astype(jnp.bfloat16)
    absorbed = jnp.einsum('rhn,hnl->rhl', queries[:, :, :NOPE].astype(jnp.float32), w_key_up.astype(jnp.float32), precision=lax.Precision.HIGHEST).astype(jnp.bfloat16)
    turned = rotate_pairs(queries[:, :, NOPE:].astype(jnp.float32), cache_lengths).astype(jnp.bfloat16)
    probes = jnp.concatenate([absorbed, turned], axis=2)
    factor = (NOPE + ROPE) ** (-0.5)
    self_score = factor * jnp.einsum('rhc,rc->rh', probes.astype(jnp.float32), new_entry.astype(jnp.float32), precision=lax.Precision.HIGHEST)
    self_weight = jnp.exp(self_score).astype(jnp.bfloat16).astype(jnp.float32)
    inverse = jnp.zeros((REQUESTS,), jnp.int32).at[request_slot].set(jnp.arange(REQUESTS, dtype=jnp.int32))
    slot_probes = probes[inverse].reshape(owners_count, REQ_DEV, HEADS, LATENT + ROPE)
    slot_lengths = cache_lengths[inverse].reshape(owners_count, REQ_DEV)
    owner_rows = latent_cache.reshape(owners_count, CACHE_DEV, LATENT + ROPE)
    numerator, denominator = lax.map(owner_attention, (slot_probes, owner_rows, slot_lengths))
    numerator = numerator.reshape(REQUESTS, HEADS, LATENT)[request_slot]
    denominator = denominator.reshape(REQUESTS, HEADS)[request_slot]
    numerator = numerator + self_weight[:, :, None] * new_entry[:, None, :LATENT].astype(jnp.float32)
    denominator = denominator + self_weight
    mixed_latent = (numerator / denominator[:, :, None]).astype(jnp.bfloat16)
    head_out = jnp.einsum('rhl,hld->rhd', mixed_latent.astype(jnp.float32), w_value_up.astype(jnp.float32), precision=lax.Precision.HIGHEST).astype(jnp.bfloat16)
    head_out = head_out.reshape(REQUESTS, HEADS * NOPE)
    attended = (wide_hidden + jnp.dot(head_out, w_out, preferred_element_type=jnp.float32)).astype(jnp.bfloat16)
    attended_wide = attended.astype(jnp.float32)
    gained = (attended_wide * ffn_gain).astype(jnp.bfloat16)
    inv_ffn = lax.rsqrt(lax.optimization_barrier(jnp.mean(attended_wide * attended_wide, axis=1)) + NORM_EPS)
    logits = jnp.dot(gained, w_router, preferred_element_type=jnp.float32) * inv_ffn[:, None]
    picked = jnp.take_along_axis(logits, routes, axis=1)
    lifted = jnp.exp(picked)
    route_weight = lifted / lax.optimization_barrier(jnp.sum(lifted, axis=1, keepdims=True))
    normed_ffn = (attended_wide * ffn_gain * inv_ffn[:, None]).astype(jnp.bfloat16)
    padded_rows = jnp.concatenate([normed_ffn, jnp.zeros((1, D), jnp.bfloat16)], axis=0)
    row_limit = owners_count * ROUTE_MOST

    def one_expert(carried, expert_id):
        member = routes == expert_id
        weight_row = lax.optimization_barrier(jnp.sum(jnp.where(member, route_weight, 0.0), axis=1))
        taken = jnp.any(member, axis=1)
        picked_rows = jnp.nonzero(taken, size=row_limit, fill_value=REQUESTS)[0].astype(jnp.int32)
        expert_in = padded_rows[picked_rows]
        gate_value = jnp.dot(expert_in, expert_gate[expert_id], preferred_element_type=jnp.float32)
        up_value = jnp.dot(expert_in, expert_up[expert_id], preferred_element_type=jnp.float32)
        activity = (jax.nn.silu(gate_value) * up_value).astype(jnp.bfloat16)
        expert_row = jnp.dot(activity, expert_down[expert_id], preferred_element_type=jnp.float32).astype(jnp.bfloat16)
        weight_pad = jnp.concatenate([weight_row, jnp.zeros((1,), jnp.float32)])[picked_rows]
        carried = carried.at[picked_rows].add(weight_pad[:, None] * expert_row.astype(jnp.float32))
        return (carried, None)
    mixture, unused = lax.scan(one_expert, jnp.zeros((REQUESTS + 1, D), jnp.float32), jnp.arange(EXPERTS, dtype=jnp.int32))
    expert_mix = mixture[:REQUESTS].astype(jnp.bfloat16)
    return (new_entry, attended, expert_mix)
```

```python
import jax
import jax.numpy as jnp
from jax import lax
from jax.sharding import PartitionSpec as P

D = 2048
NOPE = 128
ROPE = 64
LATENT = 512


NORM_EPS = 1e-06


def rotate_pairs(values, places):
    halfway = values.shape[-1] // 2
    freqs = 10000.0 ** (-jnp.arange(halfway, dtype=jnp.float32) / halfway)
    angles = places.astype(jnp.float32).reshape(places.shape + (1,) * (values.ndim - 1)) * freqs
    cosine = jnp.cos(angles)
    sine = jnp.sin(angles)
    first_half = values[..., :halfway]
    second_half = values[..., halfway:]
    return jnp.concatenate(
        [first_half * cosine - second_half * sine, first_half * sine + second_half * cosine],
        axis=-1,
    )


def owner_attend(all_heads, owner_lengths, latent_cache, head_index, factor):
    slot_rows = all_heads.shape[0]
    total_heads = all_heads.shape[1]
    probe_width = all_heads.shape[2]
    key_rows = latent_cache.shape[0]
    starts = jnp.cumsum(owner_lengths) - owner_lengths
    places = head_index * key_rows + jnp.arange(key_rows, dtype=jnp.int32)
    inside = (places[None, :] >= starts[:, None]) & (
        places[None, :] < (starts + owner_lengths)[:, None]
    )
    scores = factor * jnp.einsum(
        "qc,pc->qp",
        all_heads.reshape(slot_rows * total_heads, probe_width),
        latent_cache,
        preferred_element_type=jnp.float32,
    )
    scores = scores.reshape(slot_rows, total_heads, key_rows)
    weights = jnp.where(inside[:, None, :], jnp.exp(scores), 0.0).astype(jnp.bfloat16)
    numerator = jnp.einsum(
        "khp,pl->khl", weights, latent_cache[:, :LATENT], preferred_element_type=jnp.float32
    )
    denominator = jnp.sum(weights.astype(jnp.float32), axis=2)
    return (numerator, denominator)


def body(
    hidden,
    attn_gain,
    w_query,
    w_latent,
    w_key_up,
    w_value_up,
    w_out,
    latent_cache,
    cache_lengths,
    request_slot,
    ffn_gain,
    w_router,
    routes,
    expert_gate,
    expert_up,
    expert_down,
):
    local_rows = hidden.shape[0]
    quarter_width = hidden.shape[1]
    local_heads = w_key_up.shape[0]
    peer_count = lax.axis_size("tok")
    head_index = lax.axis_index("head")
    tok_index = lax.axis_index("tok")
    row_ids = jnp.arange(local_rows, dtype=jnp.int32)
    gathered = lax.all_gather(hidden, "head", axis=1, tiled=True)
    widened = gathered.astype(jnp.float32)
    inv_attn = lax.rsqrt(jnp.mean(widened * widened, axis=1, keepdims=True) + NORM_EPS)
    normed_attn = (widened * inv_attn * attn_gain).astype(jnp.bfloat16)
    normed_part = lax.dynamic_slice_in_dim(
        normed_attn, head_index * quarter_width, quarter_width, 1
    )
    compressed = lax.psum(
        jnp.dot(normed_part, w_latent, preferred_element_type=jnp.float32), "head"
    )
    latent_new = compressed[:, :LATENT]
    latent_new = latent_new * lax.rsqrt(
        jnp.mean(latent_new * latent_new, axis=1, keepdims=True) + NORM_EPS
    )
    new_entry = jnp.concatenate(
        [latent_new, rotate_pairs(compressed[:, LATENT:], cache_lengths)], axis=1
    ).astype(jnp.bfloat16)
    queries = jnp.dot(normed_attn, w_query, preferred_element_type=jnp.float32).astype(jnp.bfloat16)
    queries = queries.reshape(local_rows, local_heads, NOPE + ROPE)
    absorbed = jnp.einsum(
        "bhn,hnl->bhl", queries[:, :, :NOPE], w_key_up, preferred_element_type=jnp.float32
    ).astype(jnp.bfloat16)
    turned = rotate_pairs(queries[:, :, NOPE:].astype(jnp.float32), cache_lengths).astype(
        jnp.bfloat16
    )
    probes = jnp.concatenate([absorbed, turned], axis=2)
    factor = (NOPE + ROPE) ** (-0.5)
    owner_ids = jnp.arange(peer_count, dtype=jnp.int32)
    dest_owner = request_slot // local_rows
    goes_to = dest_owner[None, :] == owner_ids[:, None]
    sent_any = jnp.max(goes_to.astype(jnp.int32), axis=1)
    sent_row = jnp.sum(jnp.where(goes_to, row_ids[None, :], 0), axis=1) + local_rows * (1 - sent_any)
    packed = jnp.concatenate([probes, new_entry[:, None, :]], axis=1)
    packed = jnp.concatenate(
        [packed, jnp.zeros((1,) + packed.shape[1:], jnp.bfloat16)], axis=0
    )
    send_ints = jnp.stack(
        [
            jnp.where(sent_any > 0, request_slot[jnp.minimum(sent_row, local_rows - 1)], -1),
            cache_lengths[jnp.minimum(sent_row, local_rows - 1)],
        ],
        axis=1,
    )
    got_packed = lax.all_to_all(packed[sent_row], "tok", 0, 0, tiled=True)
    got_ints = lax.all_to_all(send_ints, "tok", 0, 0, tiled=True)
    got_slot = got_ints[:, 0]
    local_slot = got_slot - tok_index * local_rows
    slot_sel = local_slot[None, :] == row_ids[:, None]
    src_of_slot = jnp.sum(jnp.where(slot_sel, owner_ids[None, :], 0), axis=1)
    owner_packed = got_packed[src_of_slot]
    owner_probes = owner_packed[:, :local_heads]
    owner_new = owner_packed[:, local_heads]
    owner_lengths = got_ints[src_of_slot, 1]
    all_heads = lax.all_gather(owner_probes, "head", axis=1, tiled=True)
    numerator, denominator = owner_attend(
        all_heads, owner_lengths, latent_cache, head_index, factor
    )
    joined = lax.psum_scatter(
        jnp.concatenate([numerator, denominator[:, :, None]], axis=2),
        "head",
        scatter_dimension=1,
        tiled=True,
    )
    group_num = joined[:, :, :LATENT]
    group_den = joined[:, :, LATENT]
    self_score = factor * jnp.einsum(
        "bhc,bc->bh", owner_probes, owner_new, preferred_element_type=jnp.float32
    )
    self_weight = jnp.exp(self_score).astype(jnp.bfloat16).astype(jnp.float32)
    total_num = group_num + self_weight[:, :, None] * owner_new[:, None, :LATENT].astype(
        jnp.float32
    )
    total_den = group_den + self_weight
    mixed_latent = (total_num / total_den[:, :, None]).astype(jnp.bfloat16)
    owner_out = jnp.einsum(
        "bhl,hld->bhd", mixed_latent, w_value_up, preferred_element_type=jnp.float32
    ).astype(jnp.bfloat16)
    owner_out = owner_out.reshape(local_rows, local_heads * NOPE)
    owner_out = jnp.concatenate(
        [owner_out, jnp.zeros((1, local_heads * NOPE), jnp.bfloat16)], axis=0
    )
    back_valid = (local_slot >= 0) & (local_slot < local_rows)
    back_row = jnp.where(back_valid, local_slot, local_rows)
    returned_out = lax.all_to_all(owner_out[back_row], "tok", 0, 0, tiled=True)
    head_out = returned_out[dest_owner]
    head_out = head_out.reshape(local_rows, local_heads * NOPE)
    attn_piece = lax.psum_scatter(
        jnp.dot(head_out, w_out, preferred_element_type=jnp.float32),
        "head",
        scatter_dimension=1,
        tiled=True,
    )
    attended = (hidden.astype(jnp.float32) + attn_piece).astype(jnp.bfloat16)
    attended_wide = attended.astype(jnp.float32)
    gained = (attended_wide * ffn_gain).astype(jnp.bfloat16)
    squares, logit_part = lax.psum(
        (
            jnp.sum(attended_wide * attended_wide, axis=1),
            jnp.dot(gained, w_router, preferred_element_type=jnp.float32),
        ),
        "head",
    )
    inv_ffn = lax.rsqrt(squares / D + NORM_EPS)
    logits = logit_part * inv_ffn[:, None]
    normed_ffn = (attended_wide * ffn_gain * inv_ffn[:, None]).astype(jnp.bfloat16)
    expert_count = w_router.shape[1]
    route_count = routes.shape[1]
    expert_ids = jnp.arange(expert_count, dtype=jnp.int32)
    named = routes[:, :, None] == expert_ids[None, None, :]
    picked = jnp.sum(jnp.where(named, logits[:, None, :], 0.0), axis=2)
    lifted = jnp.exp(picked)
    route_weight = lifted / jnp.sum(lifted, axis=1, keepdims=True)
    struck = jnp.max(named.astype(jnp.int32), axis=1)
    earlier_hits = jnp.cumsum(struck, axis=0) - struck
    capacity = min(local_rows, max(2, 2 * local_rows * route_count // expert_count))
    route_place = routes * capacity + jnp.take_along_axis(earlier_hits, routes, axis=1)
    slot_total = expert_count * capacity
    slot_ids = jnp.arange(slot_total, dtype=jnp.int32)
    filled = route_place[None, :, :] == slot_ids[:, None, None]
    source_token = jnp.sum(
        jnp.where(filled, row_ids[None, :, None], 0), axis=(1, 2)
    ) + local_rows * (1 - jnp.max(filled.astype(jnp.int32), axis=(1, 2)))
    full_rows = lax.all_gather(normed_ffn, "head", axis=1, tiled=True)
    padded_rows = jnp.concatenate(
        [full_rows, jnp.zeros((1, full_rows.shape[1]), jnp.bfloat16)], axis=0
    )
    arrived = lax.all_to_all(
        padded_rows[source_token].reshape(expert_count, capacity, full_rows.shape[1]),
        "tok",
        split_axis=0,
        concat_axis=0,
        tiled=True,
    )
    expert_in = arrived.reshape(peer_count * capacity, full_rows.shape[1])
    gate_value = jnp.dot(expert_in, expert_gate[0], preferred_element_type=jnp.float32)
    up_value = jnp.dot(expert_in, expert_up[0], preferred_element_type=jnp.float32)
    activity = (jax.nn.silu(gate_value) * up_value).astype(jnp.bfloat16)
    expert_share = lax.psum_scatter(
        jnp.dot(activity, expert_down[0], preferred_element_type=jnp.float32).astype(jnp.bfloat16),
        "head",
        scatter_dimension=1,
        tiled=True,
    )
    returned = lax.all_to_all(
        expert_share.reshape(peer_count, capacity, quarter_width),
        "tok",
        split_axis=0,
        concat_axis=0,
        tiled=True,
    )
    chosen_rows = returned.reshape(slot_total, quarter_width)[route_place]
    expert_mix = jnp.sum(route_weight[:, :, None] * chosen_rows.astype(jnp.float32), axis=1).astype(
        jnp.bfloat16
    )
    return (new_entry, attended, expert_mix)


def solution(mesh):
    in_specs = (
        P("tok", "head"),
        P(),
        P(None, "head"),
        P("head", None),
        P("head", None, None),
        P("head", None, None),
        P("head", None),
        P(("tok", "head"), None),
        P("tok"),
        P("tok"),
        P("head"),
        P("head", None),
        P("tok", None),
        P("tok", None, "head"),
        P("tok", None, "head"),
        P("tok", "head", None),
    )
    out_specs = (P("tok", None), P("tok", "head"), P("tok", "head"))
    return jax.shard_map(body, mesh=mesh, in_specs=in_specs, out_specs=out_specs, check_vma=False)
```

```python
import jax
import jax.numpy as jnp
from jax import lax
from jax.sharding import PartitionSpec as P

D = 2048
NOPE = 128
ROPE = 64
LATENT = 512


NORM_EPS = 1e-06


def rotate_pairs(values, places):
    halfway = values.shape[-1] // 2
    freqs = 10000.0 ** (-jnp.arange(halfway, dtype=jnp.float32) / halfway)
    angles = places.astype(jnp.float32).reshape(places.shape + (1,) * (values.ndim - 1)) * freqs
    cosine = jnp.cos(angles)
    sine = jnp.sin(angles)
    first_half = values[..., :halfway]
    second_half = values[..., halfway:]
    return jnp.concatenate(
        [first_half * cosine - second_half * sine, first_half * sine + second_half * cosine],
        axis=-1,
    )


def owner_attend(all_heads, owner_lengths, latent_cache, head_index, factor):
    slot_rows = all_heads.shape[0]
    total_heads = all_heads.shape[1]
    probe_width = all_heads.shape[2]
    key_rows = latent_cache.shape[0]
    starts = jnp.cumsum(owner_lengths) - owner_lengths
    places = head_index * key_rows + jnp.arange(key_rows, dtype=jnp.int32)
    inside = (places[None, :] >= starts[:, None]) & (
        places[None, :] < (starts + owner_lengths)[:, None]
    )
    scores = factor * jnp.einsum(
        "qc,pc->qp",
        all_heads.reshape(slot_rows * total_heads, probe_width),
        latent_cache,
        preferred_element_type=jnp.float32,
    )
    scores = scores.reshape(slot_rows, total_heads, key_rows)
    weights = jnp.where(inside[:, None, :], jnp.exp(scores), 0.0).astype(jnp.bfloat16)
    numerator = jnp.einsum(
        "khp,pl->khl", weights, latent_cache[:, :LATENT], preferred_element_type=jnp.float32
    )
    denominator = jnp.sum(weights.astype(jnp.float32), axis=2)
    return (numerator, denominator)


def body(
    hidden,
    attn_gain,
    w_query,
    w_latent,
    w_key_up,
    w_value_up,
    w_out,
    latent_cache,
    cache_lengths,
    request_slot,
    ffn_gain,
    w_router,
    routes,
    expert_gate,
    expert_up,
    expert_down,
):
    local_rows = hidden.shape[0]
    quarter_width = hidden.shape[1]
    local_heads = w_key_up.shape[0]
    peer_count = lax.axis_size("tok")
    head_index = lax.axis_index("head")
    tok_index = lax.axis_index("tok")
    row_ids = jnp.arange(local_rows, dtype=jnp.int32)
    latent_width = w_latent.shape[1]
    gain_part = lax.dynamic_slice_in_dim(attn_gain, head_index * quarter_width, quarter_width, 0)
    raw_part = jnp.dot(
        (hidden.astype(jnp.float32) * gain_part).astype(jnp.bfloat16),
        w_latent,
        preferred_element_type=jnp.float32,
    )
    part_hi = lax.reduce_precision(raw_part, exponent_bits=8, mantissa_bits=7)
    rest = raw_part - part_hi
    part_mid = lax.reduce_precision(rest, exponent_bits=8, mantissa_bits=7)
    part_lo = rest - part_mid
    send_rows = jnp.concatenate(
        [
            hidden,
            part_hi.astype(jnp.bfloat16),
            part_mid.astype(jnp.bfloat16),
            part_lo.astype(jnp.bfloat16),
        ],
        axis=1,
    )
    piece_width = send_rows.shape[1]
    got_rows = lax.all_gather(send_rows, "head", axis=1, tiled=True).reshape(
        local_rows, -1, piece_width
    )
    gathered = got_rows[:, :, :quarter_width].reshape(local_rows, -1)
    got_parts = got_rows[:, :, quarter_width:].reshape(local_rows, -1, 3, latent_width).astype(
        jnp.float32
    )
    part_sums = (got_parts[:, :, 0] + got_parts[:, :, 1]) + got_parts[:, :, 2]
    widened = gathered.astype(jnp.float32)
    inv_attn = lax.rsqrt(jnp.mean(widened * widened, axis=1, keepdims=True) + NORM_EPS)
    normed_attn = (widened * inv_attn * attn_gain).astype(jnp.bfloat16)
    compressed = jnp.sum(part_sums, axis=1) * inv_attn
    latent_new = compressed[:, :LATENT]
    latent_new = latent_new * lax.rsqrt(
        jnp.mean(latent_new * latent_new, axis=1, keepdims=True) + NORM_EPS
    )
    new_entry = jnp.concatenate(
        [latent_new, rotate_pairs(compressed[:, LATENT:], cache_lengths)], axis=1
    ).astype(jnp.bfloat16)
    queries = jnp.dot(normed_attn, w_query, preferred_element_type=jnp.float32).astype(jnp.bfloat16)
    queries = queries.reshape(local_rows, local_heads, NOPE + ROPE)
    absorbed = jnp.einsum(
        "bhn,hnl->bhl", queries[:, :, :NOPE], w_key_up, preferred_element_type=jnp.float32
    ).astype(jnp.bfloat16)
    turned = rotate_pairs(queries[:, :, NOPE:].astype(jnp.float32), cache_lengths).astype(
        jnp.bfloat16
    )
    probes = jnp.concatenate([absorbed, turned], axis=2)
    factor = (NOPE + ROPE) ** (-0.5)
    self_score = factor * jnp.einsum(
        "bhc,bc->bh", probes, new_entry, preferred_element_type=jnp.float32
    )
    self_weight = jnp.exp(self_score).astype(jnp.bfloat16).astype(jnp.float32)
    owner_ids = jnp.arange(peer_count, dtype=jnp.int32)
    dest_owner = request_slot // local_rows
    goes_to = dest_owner[None, :] == owner_ids[:, None]
    sent_any = jnp.max(goes_to.astype(jnp.int32), axis=1)
    sent_row = jnp.sum(jnp.where(goes_to, row_ids[None, :], 0), axis=1)
    sent_slot = request_slot[sent_row]
    sent_len = cache_lengths[sent_row]
    code = jnp.stack(
        [sent_any, sent_slot // 64, sent_slot % 64, sent_len // 64, sent_len % 64], axis=1
    ) * sent_any[:, None]
    code_row = jnp.zeros((peer_count, probes.shape[2]), jnp.float32)
    code_row = code_row.at[:, :5].set(code.astype(jnp.float32)).astype(jnp.bfloat16)
    packed = jnp.concatenate([probes[sent_row], code_row[:, None, :]], axis=1)
    got_packed = lax.all_to_all(packed, "tok", 0, 0, tiled=True)
    got_code = got_packed[:, local_heads, :5].astype(jnp.float32).astype(jnp.int32)
    got_slot = jnp.where(got_code[:, 0] > 0, got_code[:, 1] * 64 + got_code[:, 2], -1)
    got_len = got_code[:, 3] * 64 + got_code[:, 4]
    local_slot = got_slot - tok_index * local_rows
    slot_sel = local_slot[None, :] == row_ids[:, None]
    src_of_slot = jnp.sum(jnp.where(slot_sel, owner_ids[None, :], 0), axis=1)
    owner_probes = got_packed[src_of_slot, :local_heads]
    owner_lengths = got_len[src_of_slot]
    all_heads = lax.all_gather(owner_probes, "head", axis=1, tiled=True)
    numerator, denominator = owner_attend(
        all_heads, owner_lengths, latent_cache, head_index, factor
    )
    joined = lax.psum_scatter(
        jnp.concatenate([numerator, denominator[:, :, None]], axis=2),
        "head",
        scatter_dimension=1,
        tiled=True,
    )
    joined = jnp.concatenate([joined, jnp.zeros((1,) + joined.shape[1:], jnp.float32)], axis=0)
    back_valid = (local_slot >= 0) & (local_slot < local_rows)
    back_row = jnp.where(back_valid, local_slot, local_rows)
    returned = lax.all_to_all(joined[back_row], "tok", 0, 0, tiled=True)[dest_owner]
    total_num = returned[:, :, :LATENT] + self_weight[:, :, None] * new_entry[:, None, :LATENT].astype(
        jnp.float32
    )
    total_den = returned[:, :, LATENT] + self_weight
    mixed_latent = (total_num / total_den[:, :, None]).astype(jnp.bfloat16)
    head_out = jnp.einsum(
        "bhl,hld->bhd", mixed_latent, w_value_up, preferred_element_type=jnp.float32
    ).astype(jnp.bfloat16)
    head_out = head_out.reshape(local_rows, local_heads * NOPE)
    attn_piece = lax.psum_scatter(
        jnp.dot(head_out, w_out, preferred_element_type=jnp.float32),
        "head",
        scatter_dimension=1,
        tiled=True,
    )
    attended = (hidden.astype(jnp.float32) + attn_piece).astype(jnp.bfloat16)
    attended_wide = attended.astype(jnp.float32)
    gained = (attended_wide * ffn_gain).astype(jnp.bfloat16)
    squares, logit_part = lax.psum(
        (
            jnp.sum(attended_wide * attended_wide, axis=1),
            jnp.dot(gained, w_router, preferred_element_type=jnp.float32),
        ),
        "head",
    )
    inv_ffn = lax.rsqrt(squares / D + NORM_EPS)
    logits = logit_part * inv_ffn[:, None]
    normed_ffn = (attended_wide * ffn_gain * inv_ffn[:, None]).astype(jnp.bfloat16)
    expert_count = w_router.shape[1]
    route_count = routes.shape[1]
    expert_ids = jnp.arange(expert_count, dtype=jnp.int32)
    named = routes[:, :, None] == expert_ids[None, None, :]
    picked = jnp.sum(jnp.where(named, logits[:, None, :], 0.0), axis=2)
    lifted = jnp.exp(picked)
    route_weight = lifted / jnp.sum(lifted, axis=1, keepdims=True)
    struck = jnp.max(named.astype(jnp.int32), axis=1)
    earlier_hits = jnp.cumsum(struck, axis=0) - struck
    capacity = min(local_rows, max(2, 2 * local_rows * route_count // expert_count))
    route_place = routes * capacity + jnp.take_along_axis(earlier_hits, routes, axis=1)
    slot_total = expert_count * capacity
    slot_ids = jnp.arange(slot_total, dtype=jnp.int32)
    filled = route_place[None, :, :] == slot_ids[:, None, None]
    source_token = jnp.sum(
        jnp.where(filled, row_ids[None, :, None], 0), axis=(1, 2)
    ) + local_rows * (1 - jnp.max(filled.astype(jnp.int32), axis=(1, 2)))
    padded_rows = jnp.concatenate(
        [normed_ffn, jnp.zeros((1, normed_ffn.shape[1]), jnp.bfloat16)], axis=0
    )
    arrived = lax.all_to_all(
        padded_rows[source_token].reshape(expert_count, capacity, quarter_width),
        "tok",
        split_axis=0,
        concat_axis=0,
        tiled=True,
    )
    expert_in = lax.all_gather(
        arrived.reshape(peer_count * capacity, quarter_width), "head", axis=1, tiled=True
    )
    gate_value = jnp.dot(expert_in, expert_gate[0], preferred_element_type=jnp.float32)
    up_value = jnp.dot(expert_in, expert_up[0], preferred_element_type=jnp.float32)
    activity = (jax.nn.silu(gate_value) * up_value).astype(jnp.bfloat16)
    expert_share = lax.psum_scatter(
        jnp.dot(activity, expert_down[0], preferred_element_type=jnp.float32).astype(jnp.bfloat16),
        "head",
        scatter_dimension=1,
        tiled=True,
    )
    returned = lax.all_to_all(
        expert_share.reshape(peer_count, capacity, quarter_width),
        "tok",
        split_axis=0,
        concat_axis=0,
        tiled=True,
    )
    chosen_rows = returned.reshape(slot_total, quarter_width)[route_place]
    expert_mix = jnp.sum(route_weight[:, :, None] * chosen_rows.astype(jnp.float32), axis=1).astype(
        jnp.bfloat16
    )
    return (new_entry, attended, expert_mix)


def solution(mesh):
    in_specs = (
        P("tok", "head"),
        P(),
        P(None, "head"),
        P("head", None),
        P("head", None, None),
        P("head", None, None),
        P("head", None),
        P(("tok", "head"), None),
        P("tok"),
        P("tok"),
        P("head"),
        P("head", None),
        P("tok", None),
        P("tok", None, "head"),
        P("tok", None, "head"),
        P("tok", "head", None),
    )
    out_specs = (P("tok", None), P("tok", "head"), P("tok", "head"))
    return jax.shard_map(body, mesh=mesh, in_specs=in_specs, out_specs=out_specs, check_vma=False)
```

```python
import jax
import jax.numpy as jnp
from jax import lax
from jax.sharding import PartitionSpec as P

D = 2048
NOPE = 128
ROPE = 64
LATENT = 512


NORM_EPS = 1e-06


def rotate_pairs(values, places):
    halfway = values.shape[-1] // 2
    freqs = 10000.0 ** (-jnp.arange(halfway, dtype=jnp.float32) / halfway)
    angles = places.astype(jnp.float32).reshape(places.shape + (1,) * (values.ndim - 1)) * freqs
    cosine = jnp.cos(angles)
    sine = jnp.sin(angles)
    first_half = values[..., :halfway]
    second_half = values[..., halfway:]
    return jnp.concatenate(
        [first_half * cosine - second_half * sine, first_half * sine + second_half * cosine],
        axis=-1,
    )


def owner_attend(all_heads, owner_lengths, latent_cache, head_index, factor):
    slot_rows = all_heads.shape[0]
    total_heads = all_heads.shape[1]
    probe_width = all_heads.shape[2]
    key_rows = latent_cache.shape[0]
    starts = jnp.cumsum(owner_lengths) - owner_lengths
    places = head_index * key_rows + jnp.arange(key_rows, dtype=jnp.int32)
    inside = (places[None, :] >= starts[:, None]) & (
        places[None, :] < (starts + owner_lengths)[:, None]
    )
    scores = factor * jnp.einsum(
        "qc,pc->qp",
        all_heads.reshape(slot_rows * total_heads, probe_width),
        latent_cache,
        preferred_element_type=jnp.float32,
    )
    scores = scores.reshape(slot_rows, total_heads, key_rows)
    weights = jnp.where(inside[:, None, :], jnp.exp(scores), 0.0).astype(jnp.bfloat16)
    numerator = jnp.einsum(
        "khp,pl->khl", weights, latent_cache[:, :LATENT], preferred_element_type=jnp.float32
    )
    denominator = jnp.sum(weights.astype(jnp.float32), axis=2)
    return (numerator, denominator)


def head_sum_scatter(values, axis):
    groups = lax.axis_size("head")
    moved = lax.all_to_all(values, "head", split_axis=axis, concat_axis=0, tiled=True)
    moved = moved.reshape((groups, values.shape[0]) + moved.shape[1:])
    return jnp.sum(moved.astype(jnp.float32), axis=0)


def body(
    hidden,
    attn_gain,
    w_query,
    w_latent,
    w_key_up,
    w_value_up,
    w_out,
    latent_cache,
    cache_lengths,
    request_slot,
    ffn_gain,
    w_router,
    routes,
    expert_gate,
    expert_up,
    expert_down,
):
    local_rows = hidden.shape[0]
    quarter_width = hidden.shape[1]
    local_heads = w_key_up.shape[0]
    peer_count = lax.axis_size("tok")
    head_index = lax.axis_index("head")
    tok_index = lax.axis_index("tok")
    row_ids = jnp.arange(local_rows, dtype=jnp.int32)
    latent_width = w_latent.shape[1]
    gain_part = lax.dynamic_slice_in_dim(attn_gain, head_index * quarter_width, quarter_width, 0)
    raw_part = jnp.dot(
        (hidden.astype(jnp.float32) * gain_part).astype(jnp.bfloat16),
        w_latent,
        preferred_element_type=jnp.float32,
    )
    part_hi = lax.reduce_precision(raw_part, exponent_bits=8, mantissa_bits=7)
    rest = raw_part - part_hi
    part_mid = lax.reduce_precision(rest, exponent_bits=8, mantissa_bits=7)
    part_lo = rest - part_mid
    send_rows = jnp.concatenate(
        [
            hidden,
            part_hi.astype(jnp.bfloat16),
            part_mid.astype(jnp.bfloat16),
            part_lo.astype(jnp.bfloat16),
        ],
        axis=1,
    )
    piece_width = send_rows.shape[1]
    got_rows = lax.all_gather(send_rows, "head", axis=1, tiled=True).reshape(
        local_rows, -1, piece_width
    )
    gathered = got_rows[:, :, :quarter_width].reshape(local_rows, -1)
    got_parts = got_rows[:, :, quarter_width:].reshape(local_rows, -1, 3, latent_width).astype(
        jnp.float32
    )
    part_sums = (got_parts[:, :, 0] + got_parts[:, :, 1]) + got_parts[:, :, 2]
    widened = gathered.astype(jnp.float32)
    inv_attn = lax.rsqrt(jnp.mean(widened * widened, axis=1, keepdims=True) + NORM_EPS)
    normed_attn = (widened * inv_attn * attn_gain).astype(jnp.bfloat16)
    compressed = jnp.sum(part_sums, axis=1) * inv_attn
    latent_new = compressed[:, :LATENT]
    latent_new = latent_new * lax.rsqrt(
        jnp.mean(latent_new * latent_new, axis=1, keepdims=True) + NORM_EPS
    )
    new_entry = jnp.concatenate(
        [latent_new, rotate_pairs(compressed[:, LATENT:], cache_lengths)], axis=1
    ).astype(jnp.bfloat16)
    queries = jnp.dot(normed_attn, w_query, preferred_element_type=jnp.float32).astype(jnp.bfloat16)
    queries = queries.reshape(local_rows, local_heads, NOPE + ROPE)
    absorbed = jnp.einsum(
        "bhn,hnl->bhl", queries[:, :, :NOPE], w_key_up, preferred_element_type=jnp.float32
    ).astype(jnp.bfloat16)
    turned = rotate_pairs(queries[:, :, NOPE:].astype(jnp.float32), cache_lengths).astype(
        jnp.bfloat16
    )
    probes = jnp.concatenate([absorbed, turned], axis=2)
    factor = (NOPE + ROPE) ** (-0.5)
    self_score = factor * jnp.einsum(
        "bhc,bc->bh", probes, new_entry, preferred_element_type=jnp.float32
    )
    self_weight = jnp.exp(self_score).astype(jnp.bfloat16).astype(jnp.float32)
    owner_ids = jnp.arange(peer_count, dtype=jnp.int32)
    dest_owner = request_slot // local_rows
    goes_to = dest_owner[None, :] == owner_ids[:, None]
    sent_any = jnp.max(goes_to.astype(jnp.int32), axis=1)
    sent_row = jnp.sum(jnp.where(goes_to, row_ids[None, :], 0), axis=1)
    sent_slot = request_slot[sent_row]
    sent_len = cache_lengths[sent_row]
    code = jnp.stack(
        [sent_any, sent_slot // 64, sent_slot % 64, sent_len // 64, sent_len % 64], axis=1
    ) * sent_any[:, None]
    code_row = jnp.zeros((peer_count, probes.shape[2]), jnp.float32)
    code_row = code_row.at[:, :5].set(code.astype(jnp.float32)).astype(jnp.bfloat16)
    packed = jnp.concatenate([probes[sent_row], code_row[:, None, :]], axis=1)
    got_packed = lax.all_to_all(packed, "tok", 0, 0, tiled=True)
    got_code = got_packed[:, local_heads, :5].astype(jnp.float32).astype(jnp.int32)
    got_slot = jnp.where(got_code[:, 0] > 0, got_code[:, 1] * 64 + got_code[:, 2], -1)
    got_len = got_code[:, 3] * 64 + got_code[:, 4]
    local_slot = got_slot - tok_index * local_rows
    slot_sel = local_slot[None, :] == row_ids[:, None]
    src_of_slot = jnp.sum(jnp.where(slot_sel, owner_ids[None, :], 0), axis=1)
    owner_probes = got_packed[src_of_slot, :local_heads]
    owner_lengths = got_len[src_of_slot]
    all_heads = lax.all_gather(owner_probes, "head", axis=1, tiled=True)
    numerator, denominator = owner_attend(
        all_heads, owner_lengths, latent_cache, head_index, factor
    )
    joined = head_sum_scatter(jnp.concatenate([numerator, denominator[:, :, None]], axis=2), 1)
    joined = jnp.concatenate([joined, jnp.zeros((1,) + joined.shape[1:], jnp.float32)], axis=0)
    back_valid = (local_slot >= 0) & (local_slot < local_rows)
    back_row = jnp.where(back_valid, local_slot, local_rows)
    returned = lax.all_to_all(joined[back_row], "tok", 0, 0, tiled=True)[dest_owner]
    total_num = returned[:, :, :LATENT] + self_weight[:, :, None] * new_entry[:, None, :LATENT].astype(
        jnp.float32
    )
    total_den = returned[:, :, LATENT] + self_weight
    mixed_latent = (total_num / total_den[:, :, None]).astype(jnp.bfloat16)
    head_out = jnp.einsum(
        "bhl,hld->bhd", mixed_latent, w_value_up, preferred_element_type=jnp.float32
    ).astype(jnp.bfloat16)
    head_out = head_out.reshape(local_rows, local_heads * NOPE)
    attn_piece = head_sum_scatter(jnp.dot(head_out, w_out, preferred_element_type=jnp.float32), 1)
    attended = (hidden.astype(jnp.float32) + attn_piece).astype(jnp.bfloat16)
    attended_wide = attended.astype(jnp.float32)
    gained = (attended_wide * ffn_gain).astype(jnp.bfloat16)
    squares, logit_part = lax.psum(
        (
            jnp.sum(attended_wide * attended_wide, axis=1),
            jnp.dot(gained, w_router, preferred_element_type=jnp.float32),
        ),
        "head",
    )
    inv_ffn = lax.rsqrt(squares / D + NORM_EPS)
    logits = logit_part * inv_ffn[:, None]
    normed_ffn = (attended_wide * ffn_gain * inv_ffn[:, None]).astype(jnp.bfloat16)
    expert_count = w_router.shape[1]
    route_count = routes.shape[1]
    expert_ids = jnp.arange(expert_count, dtype=jnp.int32)
    named = routes[:, :, None] == expert_ids[None, None, :]
    picked = jnp.sum(jnp.where(named, logits[:, None, :], 0.0), axis=2)
    lifted = jnp.exp(picked)
    route_weight = lifted / jnp.sum(lifted, axis=1, keepdims=True)
    struck = jnp.max(named.astype(jnp.int32), axis=1)
    earlier_hits = jnp.cumsum(struck, axis=0) - struck
    capacity = min(local_rows, max(2, 2 * local_rows * route_count // expert_count))
    route_place = routes * capacity + jnp.take_along_axis(earlier_hits, routes, axis=1)
    slot_total = expert_count * capacity
    slot_ids = jnp.arange(slot_total, dtype=jnp.int32)
    filled = route_place[None, :, :] == slot_ids[:, None, None]
    source_token = jnp.sum(
        jnp.where(filled, row_ids[None, :, None], 0), axis=(1, 2)
    ) + local_rows * (1 - jnp.max(filled.astype(jnp.int32), axis=(1, 2)))
    padded_rows = jnp.concatenate(
        [normed_ffn, jnp.zeros((1, normed_ffn.shape[1]), jnp.bfloat16)], axis=0
    )
    arrived = lax.all_to_all(
        padded_rows[source_token].reshape(expert_count, capacity, quarter_width),
        "tok",
        split_axis=0,
        concat_axis=0,
        tiled=True,
    )
    head_count = lax.axis_size("head")
    expert_in = lax.all_to_all(
        jnp.broadcast_to(
            arrived.reshape(1, peer_count * capacity, quarter_width),
            (head_count, peer_count * capacity, quarter_width),
        ),
        "head",
        split_axis=0,
        concat_axis=2,
        tiled=True,
    ).reshape(peer_count * capacity, head_count * quarter_width)
    gate_value = jnp.dot(expert_in, expert_gate[0], preferred_element_type=jnp.float32)
    up_value = jnp.dot(expert_in, expert_up[0], preferred_element_type=jnp.float32)
    activity = (jax.nn.silu(gate_value) * up_value).astype(jnp.bfloat16)
    expert_share = head_sum_scatter(
        jnp.dot(activity, expert_down[0], preferred_element_type=jnp.float32).astype(jnp.bfloat16),
        1,
    ).astype(jnp.bfloat16)
    returned = lax.all_to_all(
        expert_share.reshape(peer_count, capacity, quarter_width),
        "tok",
        split_axis=0,
        concat_axis=0,
        tiled=True,
    )
    chosen_rows = returned.reshape(slot_total, quarter_width)[route_place]
    expert_mix = jnp.sum(route_weight[:, :, None] * chosen_rows.astype(jnp.float32), axis=1).astype(
        jnp.bfloat16
    )
    return (new_entry, attended, expert_mix)


def solution(mesh):
    in_specs = (
        P("tok", "head"),
        P(),
        P(None, "head"),
        P("head", None),
        P("head", None, None),
        P("head", None, None),
        P("head", None),
        P(("tok", "head"), None),
        P("tok"),
        P("tok"),
        P("head"),
        P("head", None),
        P("tok", None),
        P("tok", None, "head"),
        P("tok", None, "head"),
        P("tok", "head", None),
    )
    out_specs = (P("tok", None), P("tok", "head"), P("tok", "head"))
    return jax.shard_map(body, mesh=mesh, in_specs=in_specs, out_specs=out_specs, check_vma=False)
```

```python
import jax
import jax.numpy as jnp
from jax import lax
from jax.sharding import PartitionSpec as P

D = 2048
NOPE = 128
ROPE = 64
LATENT = 512


NORM_EPS = 1e-06


def rotate_pairs(values, places):
    halfway = values.shape[-1] // 2
    freqs = 10000.0 ** (-jnp.arange(halfway, dtype=jnp.float32) / halfway)
    angles = places.astype(jnp.float32).reshape(places.shape + (1,) * (values.ndim - 1)) * freqs
    cosine = jnp.cos(angles)
    sine = jnp.sin(angles)
    first_half = values[..., :halfway]
    second_half = values[..., halfway:]
    return jnp.concatenate(
        [first_half * cosine - second_half * sine, first_half * sine + second_half * cosine],
        axis=-1,
    )


def owner_attend(all_heads, owner_lengths, latent_cache, head_index, factor):
    slot_rows = all_heads.shape[0]
    total_heads = all_heads.shape[1]
    probe_width = all_heads.shape[2]
    key_rows = latent_cache.shape[0]
    starts = jnp.cumsum(owner_lengths) - owner_lengths
    places = head_index * key_rows + jnp.arange(key_rows, dtype=jnp.int32)
    inside = (places[None, :] >= starts[:, None]) & (
        places[None, :] < (starts + owner_lengths)[:, None]
    )
    scores = factor * jnp.einsum(
        "qc,pc->qp",
        all_heads.reshape(slot_rows * total_heads, probe_width),
        latent_cache,
        preferred_element_type=jnp.float32,
    )
    scores = scores.reshape(slot_rows, total_heads, key_rows)
    weights = jnp.where(inside[:, None, :], jnp.exp(scores), 0.0).astype(jnp.bfloat16)
    numerator = jnp.einsum(
        "khp,pl->khl", weights, latent_cache[:, :LATENT], preferred_element_type=jnp.float32
    )
    denominator = jnp.sum(weights.astype(jnp.float32), axis=2)
    return (numerator, denominator)


def head_sum_scatter(values, axis):
    groups = lax.axis_size("head")
    moved = lax.all_to_all(values, "head", split_axis=axis, concat_axis=0, tiled=True)
    moved = moved.reshape((groups, values.shape[0]) + moved.shape[1:])
    return jnp.sum(moved.astype(jnp.float32), axis=0)


def body(
    hidden,
    attn_gain,
    w_query,
    w_latent,
    w_key_up,
    w_value_up,
    w_out,
    latent_cache,
    cache_lengths,
    request_slot,
    ffn_gain,
    w_router,
    routes,
    expert_gate,
    expert_up,
    expert_down,
):
    local_rows = hidden.shape[0]
    quarter_width = hidden.shape[1]
    local_heads = w_key_up.shape[0]
    peer_count = lax.axis_size("tok")
    head_index = lax.axis_index("head")
    tok_index = lax.axis_index("tok")
    row_ids = jnp.arange(local_rows, dtype=jnp.int32)
    latent_width = w_latent.shape[1]
    head_count = lax.axis_size("head")
    gain_part = lax.dynamic_slice_in_dim(attn_gain, head_index * quarter_width, quarter_width, 0)
    raw_part = jnp.dot(
        (hidden.astype(jnp.float32) * gain_part).astype(jnp.bfloat16),
        w_latent,
        preferred_element_type=jnp.float32,
    )
    part_width = -(-latent_width // 128) * 128
    part_hi = lax.reduce_precision(raw_part, exponent_bits=8, mantissa_bits=7)
    rest = raw_part - part_hi
    part_mid = lax.reduce_precision(rest, exponent_bits=8, mantissa_bits=7)
    part_lo = rest - part_mid
    lane_pad = jnp.zeros((local_rows, part_width - latent_width), jnp.bfloat16)
    send_rows = jnp.concatenate(
        [
            hidden,
            part_hi.astype(jnp.bfloat16),
            lane_pad,
            part_mid.astype(jnp.bfloat16),
            lane_pad,
            part_lo.astype(jnp.bfloat16),
            lane_pad,
        ],
        axis=1,
    )
    got_rows = lax.all_gather(send_rows, "head", axis=0, tiled=False)
    hidden_groups = got_rows[:, :, :quarter_width].astype(jnp.float32)

    def part_piece(k):
        offset = quarter_width + k * part_width
        return got_rows[:, :, offset : offset + latent_width].astype(jnp.float32)

    part_sums = (part_piece(0) + part_piece(1)) + part_piece(2)
    inv_attn = lax.rsqrt(
        jnp.sum(hidden_groups * hidden_groups, axis=(0, 2))[:, None] / D + NORM_EPS
    )
    normed_groups = (
        hidden_groups * inv_attn[None] * attn_gain.reshape(head_count, 1, quarter_width)
    ).astype(jnp.bfloat16)
    compressed = jnp.sum(part_sums, axis=0) * inv_attn
    latent_new = compressed[:, :LATENT]
    latent_new = latent_new * lax.rsqrt(
        jnp.mean(latent_new * latent_new, axis=1, keepdims=True) + NORM_EPS
    )
    new_entry = jnp.concatenate(
        [latent_new, rotate_pairs(compressed[:, LATENT:], cache_lengths)], axis=1
    ).astype(jnp.bfloat16)
    queries = jnp.einsum(
        "gbf,gfq->bq",
        normed_groups,
        w_query.reshape(head_count, quarter_width, w_query.shape[1]),
        preferred_element_type=jnp.float32,
    ).astype(jnp.bfloat16)
    queries = queries.reshape(local_rows, local_heads, NOPE + ROPE)
    absorbed = jnp.einsum(
        "bhn,hnl->bhl", queries[:, :, :NOPE], w_key_up, preferred_element_type=jnp.float32
    ).astype(jnp.bfloat16)
    turned = rotate_pairs(queries[:, :, NOPE:].astype(jnp.float32), cache_lengths).astype(
        jnp.bfloat16
    )
    probes = jnp.concatenate([absorbed, turned], axis=2)
    factor = (NOPE + ROPE) ** (-0.5)
    owner_ids = jnp.arange(peer_count, dtype=jnp.int32)
    dest_owner = request_slot // local_rows
    goes_to = dest_owner[None, :] == owner_ids[:, None]
    sent_any = jnp.max(goes_to.astype(jnp.int32), axis=1)
    sent_row = jnp.sum(jnp.where(goes_to, row_ids[None, :], 0), axis=1)
    sent_slot = request_slot[sent_row]
    sent_len = cache_lengths[sent_row]
    code = jnp.stack(
        [sent_any, sent_slot // 64, sent_slot % 64, sent_len // 64, sent_len % 64], axis=1
    ) * sent_any[:, None]
    code_row = jnp.zeros((peer_count, probes.shape[2]), jnp.float32)
    code_row = code_row.at[:, :5].set(code.astype(jnp.float32)).astype(jnp.bfloat16)
    packed = jnp.concatenate(
        [probes[sent_row], new_entry[sent_row][:, None, :], code_row[:, None, :]], axis=1
    )
    got_packed = lax.all_to_all(packed, "tok", 0, 0, tiled=True)
    got_code = got_packed[:, local_heads + 1, :5].astype(jnp.float32).astype(jnp.int32)
    got_slot = jnp.where(got_code[:, 0] > 0, got_code[:, 1] * 64 + got_code[:, 2], -1)
    got_len = got_code[:, 3] * 64 + got_code[:, 4]
    local_slot = got_slot - tok_index * local_rows
    slot_sel = local_slot[None, :] == row_ids[:, None]
    src_of_slot = jnp.sum(jnp.where(slot_sel, owner_ids[None, :], 0), axis=1)
    owner_probes = got_packed[src_of_slot, :local_heads]
    owner_lengths = got_len[src_of_slot]
    owner_new = got_packed[src_of_slot, local_heads]
    all_heads = lax.all_gather(owner_probes, "head", axis=1, tiled=True)
    numerator, denominator = owner_attend(
        all_heads, owner_lengths, latent_cache, head_index, factor
    )
    joined = head_sum_scatter(jnp.concatenate([numerator, denominator[:, :, None]], axis=2), 1)
    self_score = factor * jnp.einsum(
        "bhc,bc->bh", owner_probes, owner_new, preferred_element_type=jnp.float32
    )
    self_weight = jnp.exp(self_score).astype(jnp.bfloat16).astype(jnp.float32)
    total_num = joined[:, :, :LATENT] + self_weight[:, :, None] * owner_new[:, None, :LATENT].astype(
        jnp.float32
    )
    total_den = joined[:, :, LATENT] + self_weight
    mixed_latent = (total_num / total_den[:, :, None]).astype(jnp.bfloat16)
    owner_out = jnp.einsum(
        "bhl,hld->bhd", mixed_latent, w_value_up, preferred_element_type=jnp.float32
    ).astype(jnp.bfloat16)
    owner_out = owner_out.reshape(local_rows, local_heads * NOPE)
    owner_out = jnp.concatenate(
        [owner_out, jnp.zeros((1, local_heads * NOPE), jnp.bfloat16)], axis=0
    )
    back_valid = (local_slot >= 0) & (local_slot < local_rows)
    back_row = jnp.where(back_valid, local_slot, local_rows)
    head_out = lax.all_to_all(owner_out[back_row], "tok", 0, 0, tiled=True)[dest_owner]
    head_out = head_out.reshape(local_rows, local_heads * NOPE)
    attn_piece = head_sum_scatter(jnp.dot(head_out, w_out, preferred_element_type=jnp.float32), 1)
    attended = (hidden.astype(jnp.float32) + attn_piece).astype(jnp.bfloat16)
    attended_wide = attended.astype(jnp.float32)
    gained = (attended_wide * ffn_gain).astype(jnp.bfloat16)
    squares, logit_part = lax.psum(
        (
            jnp.sum(attended_wide * attended_wide, axis=1),
            jnp.dot(gained, w_router, preferred_element_type=jnp.float32),
        ),
        "head",
    )
    inv_ffn = lax.rsqrt(squares / D + NORM_EPS)
    logits = logit_part * inv_ffn[:, None]
    normed_ffn = (attended_wide * ffn_gain * inv_ffn[:, None]).astype(jnp.bfloat16)
    expert_count = w_router.shape[1]
    route_count = routes.shape[1]
    expert_ids = jnp.arange(expert_count, dtype=jnp.int32)
    named = routes[:, :, None] == expert_ids[None, None, :]
    picked = jnp.sum(jnp.where(named, logits[:, None, :], 0.0), axis=2)
    lifted = jnp.exp(picked)
    route_weight = lifted / jnp.sum(lifted, axis=1, keepdims=True)
    struck = jnp.max(named.astype(jnp.int32), axis=1)
    earlier_hits = jnp.cumsum(struck, axis=0) - struck
    capacity = min(local_rows, max(2, 2 * local_rows * route_count // expert_count))
    route_place = routes * capacity + jnp.take_along_axis(earlier_hits, routes, axis=1)
    slot_total = expert_count * capacity
    slot_ids = jnp.arange(slot_total, dtype=jnp.int32)
    filled = route_place[None, :, :] == slot_ids[:, None, None]
    source_token = jnp.sum(
        jnp.where(filled, row_ids[None, :, None], 0), axis=(1, 2)
    ) + local_rows * (1 - jnp.max(filled.astype(jnp.int32), axis=(1, 2)))
    padded_rows = jnp.concatenate(
        [normed_ffn, jnp.zeros((1, normed_ffn.shape[1]), jnp.bfloat16)], axis=0
    )
    arrived = lax.all_to_all(
        padded_rows[source_token].reshape(expert_count, capacity, quarter_width),
        "tok",
        split_axis=0,
        concat_axis=0,
        tiled=True,
    )
    expert_in = lax.all_to_all(
        jnp.broadcast_to(
            arrived.reshape(1, peer_count * capacity, quarter_width),
            (head_count, peer_count * capacity, quarter_width),
        ),
        "head",
        split_axis=0,
        concat_axis=2,
        tiled=True,
    ).reshape(peer_count * capacity, head_count * quarter_width)
    gate_value = jnp.dot(expert_in, expert_gate[0], preferred_element_type=jnp.float32)
    up_value = jnp.dot(expert_in, expert_up[0], preferred_element_type=jnp.float32)
    activity = (jax.nn.silu(gate_value) * up_value).astype(jnp.bfloat16)
    expert_share = head_sum_scatter(
        jnp.dot(activity, expert_down[0], preferred_element_type=jnp.float32).astype(jnp.bfloat16),
        1,
    ).astype(jnp.bfloat16)
    returned = lax.all_to_all(
        expert_share.reshape(peer_count, capacity, quarter_width),
        "tok",
        split_axis=0,
        concat_axis=0,
        tiled=True,
    )
    chosen_rows = returned.reshape(slot_total, quarter_width)[route_place]
    expert_mix = jnp.sum(route_weight[:, :, None] * chosen_rows.astype(jnp.float32), axis=1).astype(
        jnp.bfloat16
    )
    return (new_entry, attended, expert_mix)


def solution(mesh):
    in_specs = (
        P("tok", "head"),
        P(),
        P(None, "head"),
        P("head", None),
        P("head", None, None),
        P("head", None, None),
        P("head", None),
        P(("tok", "head"), None),
        P("tok"),
        P("tok"),
        P("head"),
        P("head", None),
        P("tok", None),
        P("tok", None, "head"),
        P("tok", None, "head"),
        P("tok", "head", None),
    )
    out_specs = (P("tok", None), P("tok", "head"), P("tok", "head"))
    return jax.shard_map(body, mesh=mesh, in_specs=in_specs, out_specs=out_specs, check_vma=False)
```

```python
import jax
import jax.numpy as jnp
from jax import lax
from jax.sharding import PartitionSpec as P

D = 2048
NOPE = 128
ROPE = 64
LATENT = 512


NORM_EPS = 1e-06


def rotate_pairs(values, places):
    halfway = values.shape[-1] // 2
    freqs = 10000.0 ** (-jnp.arange(halfway, dtype=jnp.float32) / halfway)
    angles = places.astype(jnp.float32).reshape(places.shape + (1,) * (values.ndim - 1)) * freqs
    cosine = jnp.cos(angles)
    sine = jnp.sin(angles)
    first_half = values[..., :halfway]
    second_half = values[..., halfway:]
    return jnp.concatenate(
        [first_half * cosine - second_half * sine, first_half * sine + second_half * cosine],
        axis=-1,
    )


def owner_attend(all_heads, owner_lengths, latent_cache, head_index, factor):
    slot_rows = all_heads.shape[0]
    total_heads = all_heads.shape[1]
    probe_width = all_heads.shape[2]
    key_rows = latent_cache.shape[0]
    starts = jnp.cumsum(owner_lengths) - owner_lengths
    places = head_index * key_rows + jnp.arange(key_rows, dtype=jnp.int32)
    inside = (places[None, :] >= starts[:, None]) & (
        places[None, :] < (starts + owner_lengths)[:, None]
    )
    scores = factor * jnp.einsum(
        "qc,pc->qp",
        all_heads.reshape(slot_rows * total_heads, probe_width),
        latent_cache,
        preferred_element_type=jnp.float32,
    )
    scores = scores.reshape(slot_rows, total_heads, key_rows)
    weights = jnp.where(inside[:, None, :], jnp.exp(scores), 0.0).astype(jnp.bfloat16)
    numerator = jnp.einsum(
        "khp,pl->khl", weights, latent_cache[:, :LATENT], preferred_element_type=jnp.float32
    )
    denominator = jnp.sum(weights.astype(jnp.float32), axis=2)
    return (numerator, denominator)


def head_sum_scatter(values, axis):
    groups = lax.axis_size("head")
    moved = lax.all_to_all(values, "head", split_axis=axis, concat_axis=0, tiled=True)
    moved = moved.reshape((groups, values.shape[0]) + moved.shape[1:])
    return jnp.sum(moved.astype(jnp.float32), axis=0)


def body(
    hidden,
    attn_gain,
    w_query,
    w_latent,
    w_key_up,
    w_value_up,
    w_out,
    latent_cache,
    cache_lengths,
    request_slot,
    ffn_gain,
    w_router,
    routes,
    expert_gate,
    expert_up,
    expert_down,
):
    local_rows = hidden.shape[0]
    quarter_width = hidden.shape[1]
    local_heads = w_key_up.shape[0]
    peer_count = lax.axis_size("tok")
    head_index = lax.axis_index("head")
    tok_index = lax.axis_index("tok")
    row_ids = jnp.arange(local_rows, dtype=jnp.int32)
    latent_width = w_latent.shape[1]
    head_count = lax.axis_size("head")
    gain_part = lax.dynamic_slice_in_dim(attn_gain, head_index * quarter_width, quarter_width, 0)
    raw_part = jnp.dot(
        (hidden.astype(jnp.float32) * gain_part).astype(jnp.bfloat16),
        w_latent,
        preferred_element_type=jnp.float32,
    )
    part_width = -(-latent_width // 128) * 128
    part_hi = lax.reduce_precision(raw_part, exponent_bits=8, mantissa_bits=7)
    rest = raw_part - part_hi
    part_mid = lax.reduce_precision(rest, exponent_bits=8, mantissa_bits=7)
    part_lo = rest - part_mid
    lane_pad = jnp.zeros((local_rows, part_width - latent_width), jnp.bfloat16)
    send_rows = jnp.concatenate(
        [
            hidden,
            part_hi.astype(jnp.bfloat16),
            lane_pad,
            part_mid.astype(jnp.bfloat16),
            lane_pad,
            part_lo.astype(jnp.bfloat16),
            lane_pad,
        ],
        axis=1,
    )
    gain_hi = lax.reduce_precision(ffn_gain, exponent_bits=8, mantissa_bits=7)
    gain_rest = ffn_gain - gain_hi
    gain_mid = lax.reduce_precision(gain_rest, exponent_bits=8, mantissa_bits=7)
    gain_lo = gain_rest - gain_mid
    gain_rows = jnp.zeros((8, send_rows.shape[1]), jnp.bfloat16)
    gain_rows = gain_rows.at[:3, :quarter_width].set(
        jnp.stack([gain_hi, gain_mid, gain_lo]).astype(jnp.bfloat16)
    )
    got_all = lax.all_gather(
        jnp.concatenate([send_rows, gain_rows], axis=0), "head", axis=0, tiled=False
    )
    got_rows = got_all[:, :local_rows]
    got_gain = got_all[:, local_rows : local_rows + 3, :quarter_width].astype(jnp.float32)
    gain_full = ((got_gain[:, 0] + got_gain[:, 1]) + got_gain[:, 2]).reshape(-1)
    hidden_groups = got_rows[:, :, :quarter_width].astype(jnp.float32)

    def part_piece(k):
        offset = quarter_width + k * part_width
        return got_rows[:, :, offset : offset + latent_width].astype(jnp.float32)

    part_sums = (part_piece(0) + part_piece(1)) + part_piece(2)
    inv_attn = lax.rsqrt(
        jnp.sum(hidden_groups * hidden_groups, axis=(0, 2))[:, None] / D + NORM_EPS
    )
    normed_groups = (
        hidden_groups * inv_attn[None] * attn_gain.reshape(head_count, 1, quarter_width)
    ).astype(jnp.bfloat16)
    compressed = jnp.sum(part_sums, axis=0) * inv_attn
    latent_new = compressed[:, :LATENT]
    latent_new = latent_new * lax.rsqrt(
        jnp.mean(latent_new * latent_new, axis=1, keepdims=True) + NORM_EPS
    )
    new_entry = jnp.concatenate(
        [latent_new, rotate_pairs(compressed[:, LATENT:], cache_lengths)], axis=1
    ).astype(jnp.bfloat16)
    queries = jnp.einsum(
        "gbf,gfq->bq",
        normed_groups,
        w_query.reshape(head_count, quarter_width, w_query.shape[1]),
        preferred_element_type=jnp.float32,
    ).astype(jnp.bfloat16)
    queries = queries.reshape(local_rows, local_heads, NOPE + ROPE)
    absorbed = jnp.einsum(
        "bhn,hnl->bhl", queries[:, :, :NOPE], w_key_up, preferred_element_type=jnp.float32
    ).astype(jnp.bfloat16)
    turned = rotate_pairs(queries[:, :, NOPE:].astype(jnp.float32), cache_lengths).astype(
        jnp.bfloat16
    )
    probes = jnp.concatenate([absorbed, turned], axis=2)
    factor = (NOPE + ROPE) ** (-0.5)
    owner_ids = jnp.arange(peer_count, dtype=jnp.int32)
    dest_owner = request_slot // local_rows
    goes_to = dest_owner[None, :] == owner_ids[:, None]
    sent_any = jnp.max(goes_to.astype(jnp.int32), axis=1)
    sent_row = jnp.sum(jnp.where(goes_to, row_ids[None, :], 0), axis=1)
    sent_slot = request_slot[sent_row]
    sent_len = cache_lengths[sent_row]
    code = jnp.stack(
        [sent_any, sent_slot // 64, sent_slot % 64, sent_len // 64, sent_len % 64], axis=1
    ) * sent_any[:, None]
    code_row = jnp.zeros((peer_count, probes.shape[2]), jnp.float32)
    code_row = code_row.at[:, :5].set(code.astype(jnp.float32)).astype(jnp.bfloat16)
    packed = jnp.concatenate(
        [probes[sent_row], new_entry[sent_row][:, None, :], code_row[:, None, :]], axis=1
    )
    got_packed = lax.all_to_all(packed, "tok", 0, 0, tiled=True)
    got_code = got_packed[:, local_heads + 1, :5].astype(jnp.float32).astype(jnp.int32)
    got_slot = jnp.where(got_code[:, 0] > 0, got_code[:, 1] * 64 + got_code[:, 2], -1)
    got_len = got_code[:, 3] * 64 + got_code[:, 4]
    local_slot = got_slot - tok_index * local_rows
    slot_sel = local_slot[None, :] == row_ids[:, None]
    src_of_slot = jnp.sum(jnp.where(slot_sel, owner_ids[None, :], 0), axis=1)
    owner_probes = got_packed[src_of_slot, :local_heads]
    owner_lengths = got_len[src_of_slot]
    owner_new = got_packed[src_of_slot, local_heads]
    all_heads = lax.all_gather(owner_probes, "head", axis=1, tiled=True)
    numerator, denominator = owner_attend(
        all_heads, owner_lengths, latent_cache, head_index, factor
    )
    joined = head_sum_scatter(jnp.concatenate([numerator, denominator[:, :, None]], axis=2), 1)
    self_score = factor * jnp.einsum(
        "bhc,bc->bh", owner_probes, owner_new, preferred_element_type=jnp.float32
    )
    self_weight = jnp.exp(self_score).astype(jnp.bfloat16).astype(jnp.float32)
    total_num = joined[:, :, :LATENT] + self_weight[:, :, None] * owner_new[:, None, :LATENT].astype(
        jnp.float32
    )
    total_den = joined[:, :, LATENT] + self_weight
    mixed_latent = (total_num / total_den[:, :, None]).astype(jnp.bfloat16)
    owner_out = jnp.einsum(
        "bhl,hld->bhd", mixed_latent, w_value_up, preferred_element_type=jnp.float32
    ).astype(jnp.bfloat16)
    owner_out = owner_out.reshape(local_rows, local_heads * NOPE)
    owner_out = jnp.concatenate(
        [owner_out, jnp.zeros((1, local_heads * NOPE), jnp.bfloat16)], axis=0
    )
    back_valid = (local_slot >= 0) & (local_slot < local_rows)
    back_row = jnp.where(back_valid, local_slot, local_rows)
    head_out = lax.all_to_all(owner_out[back_row], "tok", 0, 0, tiled=True)[dest_owner]
    head_out = head_out.reshape(local_rows, local_heads * NOPE)
    attn_piece = head_sum_scatter(jnp.dot(head_out, w_out, preferred_element_type=jnp.float32), 1)
    attended = (hidden.astype(jnp.float32) + attn_piece).astype(jnp.bfloat16)
    attended_wide = attended.astype(jnp.float32)
    gained = (attended_wide * ffn_gain).astype(jnp.bfloat16)
    stats = lax.psum(
        jnp.concatenate(
            [
                jnp.sum(attended_wide * attended_wide, axis=1, keepdims=True),
                jnp.dot(gained, w_router, preferred_element_type=jnp.float32),
            ],
            axis=1,
        ),
        "head",
    )
    inv_ffn = lax.rsqrt(stats[:, 0] / D + NORM_EPS)
    logits = stats[:, 1:] * inv_ffn[:, None]
    expert_count = w_router.shape[1]
    route_count = routes.shape[1]
    expert_ids = jnp.arange(expert_count, dtype=jnp.int32)
    named = routes[:, :, None] == expert_ids[None, None, :]
    picked = jnp.sum(jnp.where(named, logits[:, None, :], 0.0), axis=2)
    lifted = jnp.exp(picked)
    route_weight = lifted / jnp.sum(lifted, axis=1, keepdims=True)
    struck = jnp.max(named.astype(jnp.int32), axis=1)
    earlier_hits = jnp.cumsum(struck, axis=0) - struck
    capacity = min(local_rows, max(2, 2 * local_rows * route_count // expert_count))
    route_place = routes * capacity + jnp.take_along_axis(earlier_hits, routes, axis=1)
    slot_total = expert_count * capacity
    slot_ids = jnp.arange(slot_total, dtype=jnp.int32)
    filled = route_place[None, :, :] == slot_ids[:, None, None]
    source_token = jnp.sum(
        jnp.where(filled, row_ids[None, :, None], 0), axis=(1, 2)
    ) + local_rows * (1 - jnp.max(filled.astype(jnp.int32), axis=(1, 2)))
    padded_rows = jnp.concatenate(
        [attended, jnp.zeros((1, attended.shape[1]), jnp.bfloat16)], axis=0
    )
    arrived = lax.all_to_all(
        padded_rows[source_token].reshape(expert_count, capacity, quarter_width),
        "tok",
        split_axis=0,
        concat_axis=0,
        tiled=True,
    )
    expert_in = lax.all_to_all(
        jnp.broadcast_to(
            arrived.reshape(1, peer_count * capacity, quarter_width),
            (head_count, peer_count * capacity, quarter_width),
        ),
        "head",
        split_axis=0,
        concat_axis=2,
        tiled=True,
    ).reshape(peer_count * capacity, head_count * quarter_width)
    expert_wide = expert_in.astype(jnp.float32)
    expert_inv = lax.rsqrt(jnp.mean(expert_wide * expert_wide, axis=1, keepdims=True) + NORM_EPS)
    expert_in = (expert_wide * gain_full * expert_inv).astype(jnp.bfloat16)
    gate_value = jnp.dot(expert_in, expert_gate[0], preferred_element_type=jnp.float32)
    up_value = jnp.dot(expert_in, expert_up[0], preferred_element_type=jnp.float32)
    activity = (jax.nn.silu(gate_value) * up_value).astype(jnp.bfloat16)
    expert_share = head_sum_scatter(
        jnp.dot(activity, expert_down[0], preferred_element_type=jnp.float32).astype(jnp.bfloat16),
        1,
    ).astype(jnp.bfloat16)
    returned = lax.all_to_all(
        expert_share.reshape(peer_count, capacity, quarter_width),
        "tok",
        split_axis=0,
        concat_axis=0,
        tiled=True,
    )
    chosen_rows = returned.reshape(slot_total, quarter_width)[route_place]
    expert_mix = jnp.sum(route_weight[:, :, None] * chosen_rows.astype(jnp.float32), axis=1).astype(
        jnp.bfloat16
    )
    return (new_entry, attended, expert_mix)


def solution(mesh):
    in_specs = (
        P("tok", "head"),
        P(),
        P(None, "head"),
        P("head", None),
        P("head", None, None),
        P("head", None, None),
        P("head", None),
        P(("tok", "head"), None),
        P("tok"),
        P("tok"),
        P("head"),
        P("head", None),
        P("tok", None),
        P("tok", None, "head"),
        P("tok", None, "head"),
        P("tok", "head", None),
    )
    out_specs = (P("tok", None), P("tok", "head"), P("tok", "head"))
    return jax.shard_map(body, mesh=mesh, in_specs=in_specs, out_specs=out_specs, check_vma=False)
```

```python
import jax
import jax.numpy as jnp
from jax import lax
from jax.sharding import PartitionSpec as P

D = 2048
NOPE = 128
ROPE = 64
LATENT = 512


NORM_EPS = 1e-06


def rotate_pairs(values, places):
    halfway = values.shape[-1] // 2
    freqs = 10000.0 ** (-jnp.arange(halfway, dtype=jnp.float32) / halfway)
    angles = places.astype(jnp.float32).reshape(places.shape + (1,) * (values.ndim - 1)) * freqs
    cosine = jnp.cos(angles)
    sine = jnp.sin(angles)
    first_half = values[..., :halfway]
    second_half = values[..., halfway:]
    return jnp.concatenate(
        [first_half * cosine - second_half * sine, first_half * sine + second_half * cosine],
        axis=-1,
    )


def owner_attend(all_heads, owner_lengths, latent_cache, head_index, factor):
    slot_rows = all_heads.shape[0]
    total_heads = all_heads.shape[1]
    probe_width = all_heads.shape[2]
    key_rows = latent_cache.shape[0]
    starts = jnp.cumsum(owner_lengths) - owner_lengths
    places = head_index * key_rows + jnp.arange(key_rows, dtype=jnp.int32)
    inside = (places[None, :] >= starts[:, None]) & (
        places[None, :] < (starts + owner_lengths)[:, None]
    )
    scores = factor * jnp.einsum(
        "qc,pc->qp",
        all_heads.reshape(slot_rows * total_heads, probe_width),
        latent_cache,
        preferred_element_type=jnp.float32,
    )
    scores = scores.reshape(slot_rows, total_heads, key_rows)
    weights = jnp.where(inside[:, None, :], jnp.exp(scores), 0.0).astype(jnp.bfloat16)
    numerator = jnp.einsum(
        "khp,pl->khl", weights, latent_cache[:, :LATENT], preferred_element_type=jnp.float32
    )
    denominator = jnp.sum(weights.astype(jnp.float32), axis=2)
    return (numerator, denominator)


def head_sum_scatter(values, axis):
    groups = lax.axis_size("head")
    moved = lax.all_to_all(values, "head", split_axis=axis, concat_axis=0, tiled=True)
    moved = moved.reshape((groups, values.shape[0]) + moved.shape[1:])
    return jnp.sum(moved.astype(jnp.float32), axis=0)


def body(
    hidden,
    attn_gain,
    w_query,
    w_latent,
    w_key_up,
    w_value_up,
    w_out,
    latent_cache,
    cache_lengths,
    request_slot,
    ffn_gain,
    w_router,
    routes,
    expert_gate,
    expert_up,
    expert_down,
):
    local_rows = hidden.shape[0]
    quarter_width = hidden.shape[1]
    local_heads = w_key_up.shape[0]
    peer_count = lax.axis_size("tok")
    head_index = lax.axis_index("head")
    tok_index = lax.axis_index("tok")
    row_ids = jnp.arange(local_rows, dtype=jnp.int32)
    latent_width = w_latent.shape[1]
    head_count = lax.axis_size("head")
    gain_part = lax.dynamic_slice_in_dim(attn_gain, head_index * quarter_width, quarter_width, 0)
    raw_part = jnp.dot(
        (hidden.astype(jnp.float32) * gain_part).astype(jnp.bfloat16),
        w_latent,
        preferred_element_type=jnp.float32,
    )
    part_width = -(-latent_width // 128) * 128
    part_hi = lax.reduce_precision(raw_part, exponent_bits=8, mantissa_bits=7)
    rest = raw_part - part_hi
    part_mid = lax.reduce_precision(rest, exponent_bits=8, mantissa_bits=7)
    part_lo = rest - part_mid
    lane_pad = jnp.zeros((local_rows, part_width - latent_width), jnp.bfloat16)
    send_rows = jnp.concatenate(
        [
            hidden,
            part_hi.astype(jnp.bfloat16),
            lane_pad,
            part_mid.astype(jnp.bfloat16),
            lane_pad,
            part_lo.astype(jnp.bfloat16),
            lane_pad,
        ],
        axis=1,
    )
    gain_hi = lax.reduce_precision(ffn_gain, exponent_bits=8, mantissa_bits=7)
    gain_rest = ffn_gain - gain_hi
    gain_mid = lax.reduce_precision(gain_rest, exponent_bits=8, mantissa_bits=7)
    gain_lo = gain_rest - gain_mid
    gain_rows = jnp.zeros((8, send_rows.shape[1]), jnp.bfloat16)
    router_column = lax.dynamic_index_in_dim(w_router, tok_index, axis=1, keepdims=False)
    gain_rows = gain_rows.at[:4, :quarter_width].set(
        jnp.concatenate(
            [jnp.stack([gain_hi, gain_mid, gain_lo]).astype(jnp.bfloat16), router_column[None]],
            axis=0,
        )
    )
    got_all = lax.all_gather(
        jnp.concatenate([send_rows, gain_rows], axis=0), "head", axis=0, tiled=False
    )
    got_rows = got_all[:, :local_rows]
    got_gain = got_all[:, local_rows : local_rows + 3, :quarter_width].astype(jnp.float32)
    gain_full = ((got_gain[:, 0] + got_gain[:, 1]) + got_gain[:, 2]).reshape(-1)
    expert_column = got_all[:, local_rows + 3, :quarter_width].reshape(-1)
    hidden_groups = got_rows[:, :, :quarter_width].astype(jnp.float32)

    def part_piece(k):
        offset = quarter_width + k * part_width
        return got_rows[:, :, offset : offset + latent_width].astype(jnp.float32)

    part_sums = (part_piece(0) + part_piece(1)) + part_piece(2)
    inv_attn = lax.rsqrt(
        jnp.sum(hidden_groups * hidden_groups, axis=(0, 2))[:, None] / D + NORM_EPS
    )
    normed_groups = (
        hidden_groups * inv_attn[None] * attn_gain.reshape(head_count, 1, quarter_width)
    ).astype(jnp.bfloat16)
    compressed = jnp.sum(part_sums, axis=0) * inv_attn
    latent_new = compressed[:, :LATENT]
    latent_new = latent_new * lax.rsqrt(
        jnp.mean(latent_new * latent_new, axis=1, keepdims=True) + NORM_EPS
    )
    new_entry = jnp.concatenate(
        [latent_new, rotate_pairs(compressed[:, LATENT:], cache_lengths)], axis=1
    ).astype(jnp.bfloat16)
    queries = jnp.einsum(
        "gbf,gfq->bq",
        normed_groups,
        w_query.reshape(head_count, quarter_width, w_query.shape[1]),
        preferred_element_type=jnp.float32,
    ).astype(jnp.bfloat16)
    queries = queries.reshape(local_rows, local_heads, NOPE + ROPE)
    absorbed = jnp.einsum(
        "bhn,hnl->bhl", queries[:, :, :NOPE], w_key_up, preferred_element_type=jnp.float32
    ).astype(jnp.bfloat16)
    turned = rotate_pairs(queries[:, :, NOPE:].astype(jnp.float32), cache_lengths).astype(
        jnp.bfloat16
    )
    probes = jnp.concatenate([absorbed, turned], axis=2)
    factor = (NOPE + ROPE) ** (-0.5)
    owner_ids = jnp.arange(peer_count, dtype=jnp.int32)
    dest_owner = request_slot // local_rows
    goes_to = dest_owner[None, :] == owner_ids[:, None]
    sent_any = jnp.max(goes_to.astype(jnp.int32), axis=1)
    sent_row = jnp.sum(jnp.where(goes_to, row_ids[None, :], 0), axis=1)
    sent_slot = request_slot[sent_row]
    sent_len = cache_lengths[sent_row]
    code = jnp.stack(
        [sent_any, sent_slot // 64, sent_slot % 64, sent_len // 64, sent_len % 64], axis=1
    ) * sent_any[:, None]
    code_row = jnp.zeros((peer_count, probes.shape[2]), jnp.float32)
    code_row = code_row.at[:, :5].set(code.astype(jnp.float32)).astype(jnp.bfloat16)
    packed = jnp.concatenate(
        [probes[sent_row], new_entry[sent_row][:, None, :], code_row[:, None, :]], axis=1
    )
    got_packed = lax.all_to_all(packed, "tok", 0, 0, tiled=True)
    got_code = got_packed[:, local_heads + 1, :5].astype(jnp.float32).astype(jnp.int32)
    got_slot = jnp.where(got_code[:, 0] > 0, got_code[:, 1] * 64 + got_code[:, 2], -1)
    got_len = got_code[:, 3] * 64 + got_code[:, 4]
    local_slot = got_slot - tok_index * local_rows
    slot_sel = local_slot[None, :] == row_ids[:, None]
    src_of_slot = jnp.sum(jnp.where(slot_sel, owner_ids[None, :], 0), axis=1)
    owner_probes = got_packed[src_of_slot, :local_heads]
    owner_lengths = got_len[src_of_slot]
    owner_new = got_packed[src_of_slot, local_heads]
    all_heads = lax.all_gather(owner_probes, "head", axis=1, tiled=True)
    numerator, denominator = owner_attend(
        all_heads, owner_lengths, latent_cache, head_index, factor
    )
    joined = head_sum_scatter(jnp.concatenate([numerator, denominator[:, :, None]], axis=2), 1)
    self_score = factor * jnp.einsum(
        "bhc,bc->bh", owner_probes, owner_new, preferred_element_type=jnp.float32
    )
    self_weight = jnp.exp(self_score).astype(jnp.bfloat16).astype(jnp.float32)
    total_num = joined[:, :, :LATENT] + self_weight[:, :, None] * owner_new[:, None, :LATENT].astype(
        jnp.float32
    )
    total_den = joined[:, :, LATENT] + self_weight
    mixed_latent = (total_num / total_den[:, :, None]).astype(jnp.bfloat16)
    owner_out = jnp.einsum(
        "bhl,hld->bhd", mixed_latent, w_value_up, preferred_element_type=jnp.float32
    ).astype(jnp.bfloat16)
    owner_out = owner_out.reshape(local_rows, local_heads * NOPE)
    owner_out = jnp.concatenate(
        [owner_out, jnp.zeros((1, local_heads * NOPE), jnp.bfloat16)], axis=0
    )
    back_valid = (local_slot >= 0) & (local_slot < local_rows)
    back_row = jnp.where(back_valid, local_slot, local_rows)
    head_out = lax.all_to_all(owner_out[back_row], "tok", 0, 0, tiled=True)[dest_owner]
    head_out = head_out.reshape(local_rows, local_heads * NOPE)
    attn_piece = head_sum_scatter(jnp.dot(head_out, w_out, preferred_element_type=jnp.float32), 1)
    attended = (hidden.astype(jnp.float32) + attn_piece).astype(jnp.bfloat16)
    attended_wide = attended.astype(jnp.float32)
    expert_count = w_router.shape[1]
    route_count = routes.shape[1]
    expert_ids = jnp.arange(expert_count, dtype=jnp.int32)
    named = routes[:, :, None] == expert_ids[None, None, :]
    struck = jnp.max(named.astype(jnp.int32), axis=1)
    earlier_hits = jnp.cumsum(struck, axis=0) - struck
    capacity = min(local_rows, max(2, 2 * local_rows * route_count // expert_count))
    route_place = routes * capacity + jnp.take_along_axis(earlier_hits, routes, axis=1)
    slot_total = expert_count * capacity
    slot_ids = jnp.arange(slot_total, dtype=jnp.int32)
    filled = route_place[None, :, :] == slot_ids[:, None, None]
    source_token = jnp.sum(
        jnp.where(filled, row_ids[None, :, None], 0), axis=(1, 2)
    ) + local_rows * (1 - jnp.max(filled.astype(jnp.int32), axis=(1, 2)))
    padded_rows = jnp.concatenate(
        [attended, jnp.zeros((1, attended.shape[1]), jnp.bfloat16)], axis=0
    )
    arrived = lax.all_to_all(
        padded_rows[source_token].reshape(expert_count, capacity, quarter_width),
        "tok",
        split_axis=0,
        concat_axis=0,
        tiled=True,
    )
    expert_in = lax.all_to_all(
        jnp.broadcast_to(
            arrived.reshape(1, peer_count * capacity, quarter_width),
            (head_count, peer_count * capacity, quarter_width),
        ),
        "head",
        split_axis=0,
        concat_axis=2,
        tiled=True,
    ).reshape(peer_count * capacity, head_count * quarter_width)
    expert_wide = expert_in.astype(jnp.float32)
    expert_inv = lax.rsqrt(jnp.mean(expert_wide * expert_wide, axis=1, keepdims=True) + NORM_EPS)
    expert_gained = (expert_wide * gain_full).astype(jnp.bfloat16)
    expert_logit = (
        jnp.dot(expert_gained, expert_column, preferred_element_type=jnp.float32)
        * expert_inv[:, 0]
    )
    expert_in = (expert_wide * gain_full * expert_inv).astype(jnp.bfloat16)
    gate_value = jnp.dot(expert_in, expert_gate[0], preferred_element_type=jnp.float32)
    up_value = jnp.dot(expert_in, expert_up[0], preferred_element_type=jnp.float32)
    activity = (jax.nn.silu(gate_value) * up_value).astype(jnp.bfloat16)
    expert_share = head_sum_scatter(
        jnp.dot(activity, expert_down[0], preferred_element_type=jnp.float32).astype(jnp.bfloat16),
        1,
    ).astype(jnp.bfloat16)
    logit_hi = lax.reduce_precision(expert_logit, exponent_bits=8, mantissa_bits=7)
    logit_rest = expert_logit - logit_hi
    logit_mid = lax.reduce_precision(logit_rest, exponent_bits=8, mantissa_bits=7)
    logit_lo = logit_rest - logit_mid
    logit_code = jnp.stack([logit_hi, logit_mid, logit_lo], axis=1).reshape(
        peer_count, capacity * 3
    )
    logit_row = jnp.zeros((peer_count, 1, quarter_width), jnp.float32)
    logit_row = logit_row.at[:, 0, : capacity * 3].set(logit_code).astype(jnp.bfloat16)
    returned = lax.all_to_all(
        jnp.concatenate(
            [expert_share.reshape(peer_count, capacity, quarter_width), logit_row], axis=1
        ),
        "tok",
        split_axis=0,
        concat_axis=0,
        tiled=True,
    )
    chosen_rows = returned[:, :capacity].reshape(slot_total, quarter_width)[route_place]
    got_logit = returned[:, capacity, : capacity * 3].reshape(slot_total, 3).astype(jnp.float32)
    slot_logit = (got_logit[:, 0] + got_logit[:, 1]) + got_logit[:, 2]
    picked = slot_logit[route_place]
    lifted = jnp.exp(picked)
    route_weight = lifted / jnp.sum(lifted, axis=1, keepdims=True)
    expert_mix = jnp.sum(route_weight[:, :, None] * chosen_rows.astype(jnp.float32), axis=1).astype(
        jnp.bfloat16
    )
    return (new_entry, attended, expert_mix)


def solution(mesh):
    in_specs = (
        P("tok", "head"),
        P(),
        P(None, "head"),
        P("head", None),
        P("head", None, None),
        P("head", None, None),
        P("head", None),
        P(("tok", "head"), None),
        P("tok"),
        P("tok"),
        P("head"),
        P("head", None),
        P("tok", None),
        P("tok", None, "head"),
        P("tok", None, "head"),
        P("tok", "head", None),
    )
    out_specs = (P("tok", None), P("tok", "head"), P("tok", "head"))
    return jax.shard_map(body, mesh=mesh, in_specs=in_specs, out_specs=out_specs, check_vma=False)
```

```python
import jax
import jax.numpy as jnp
from jax import lax
from jax.sharding import PartitionSpec as P

D = 2048
NOPE = 128
ROPE = 64
LATENT = 512


NORM_EPS = 1e-06


def rotate_pairs(values, places):
    halfway = values.shape[-1] // 2
    freqs = 10000.0 ** (-jnp.arange(halfway, dtype=jnp.float32) / halfway)
    angles = places.astype(jnp.float32).reshape(places.shape + (1,) * (values.ndim - 1)) * freqs
    cosine = jnp.cos(angles)
    sine = jnp.sin(angles)
    first_half = values[..., :halfway]
    second_half = values[..., halfway:]
    return jnp.concatenate(
        [first_half * cosine - second_half * sine, first_half * sine + second_half * cosine],
        axis=-1,
    )


def owner_attend(grouped_heads, owner_lengths, latent_cache, head_index, factor):
    groups, slot_rows, group_heads, probe_width = grouped_heads.shape
    key_rows = latent_cache.shape[0]
    starts = jnp.cumsum(owner_lengths) - owner_lengths
    places = head_index * key_rows + jnp.arange(key_rows, dtype=jnp.int32)
    inside = (places[None, :] >= starts[:, None]) & (
        places[None, :] < (starts + owner_lengths)[:, None]
    )
    scores = factor * jnp.einsum(
        "qc,pc->qp",
        grouped_heads.reshape(-1, probe_width),
        latent_cache,
        preferred_element_type=jnp.float32,
    )
    scores = scores.reshape(groups, slot_rows, group_heads, key_rows)
    weights = jnp.where(inside[None, :, None, :], jnp.exp(scores), 0.0).astype(jnp.bfloat16)
    numerator = jnp.einsum(
        "qp,pl->ql",
        weights.reshape(-1, key_rows),
        latent_cache[:, :LATENT],
        preferred_element_type=jnp.float32,
    ).reshape(groups, slot_rows, group_heads, LATENT)
    denominator = jnp.sum(weights.astype(jnp.float32), axis=3)
    return (numerator, denominator)


def head_sum_scatter(grouped):
    moved = lax.all_to_all(grouped, "head", split_axis=0, concat_axis=0, tiled=True)
    return jnp.sum(moved.astype(jnp.float32), axis=0)


def body(
    hidden,
    attn_gain,
    w_query,
    w_latent,
    w_key_up,
    w_value_up,
    w_out,
    latent_cache,
    cache_lengths,
    request_slot,
    ffn_gain,
    w_router,
    routes,
    expert_gate,
    expert_up,
    expert_down,
):
    local_rows = hidden.shape[0]
    quarter_width = hidden.shape[1]
    local_heads = w_key_up.shape[0]
    peer_count = lax.axis_size("tok")
    head_index = lax.axis_index("head")
    tok_index = lax.axis_index("tok")
    row_ids = jnp.arange(local_rows, dtype=jnp.int32)
    latent_width = w_latent.shape[1]
    head_count = lax.axis_size("head")
    gain_part = lax.dynamic_slice_in_dim(attn_gain, head_index * quarter_width, quarter_width, 0)
    raw_part = jnp.dot(
        (hidden.astype(jnp.float32) * gain_part).astype(jnp.bfloat16),
        w_latent,
        preferred_element_type=jnp.float32,
    )
    part_width = -(-latent_width // 128) * 128
    part_hi = lax.reduce_precision(raw_part, exponent_bits=8, mantissa_bits=7)
    rest = raw_part - part_hi
    part_mid = lax.reduce_precision(rest, exponent_bits=8, mantissa_bits=7)
    part_lo = rest - part_mid
    lane_pad = jnp.zeros((local_rows, part_width - latent_width), jnp.bfloat16)
    send_rows = jnp.concatenate(
        [
            hidden,
            part_hi.astype(jnp.bfloat16),
            lane_pad,
            part_mid.astype(jnp.bfloat16),
            lane_pad,
            part_lo.astype(jnp.bfloat16),
            lane_pad,
        ],
        axis=1,
    )
    gain_hi = lax.reduce_precision(ffn_gain, exponent_bits=8, mantissa_bits=7)
    gain_rest = ffn_gain - gain_hi
    gain_mid = lax.reduce_precision(gain_rest, exponent_bits=8, mantissa_bits=7)
    gain_lo = gain_rest - gain_mid
    gain_rows = jnp.zeros((8, send_rows.shape[1]), jnp.bfloat16)
    router_column = lax.dynamic_index_in_dim(w_router, tok_index, axis=1, keepdims=False)
    gain_rows = gain_rows.at[:4, :quarter_width].set(
        jnp.concatenate(
            [jnp.stack([gain_hi, gain_mid, gain_lo]).astype(jnp.bfloat16), router_column[None]],
            axis=0,
        )
    )
    got_all = lax.all_gather(
        jnp.concatenate([send_rows, gain_rows], axis=0), "head", axis=0, tiled=False
    )
    got_rows = got_all[:, :local_rows]
    got_gain = got_all[:, local_rows : local_rows + 3, :quarter_width].astype(jnp.float32)
    gain_full = ((got_gain[:, 0] + got_gain[:, 1]) + got_gain[:, 2]).reshape(-1)
    expert_column = got_all[:, local_rows + 3, :quarter_width].reshape(-1)
    hidden_groups = got_rows[:, :, :quarter_width].astype(jnp.float32)

    def part_piece(k):
        offset = quarter_width + k * part_width
        return got_rows[:, :, offset : offset + latent_width].astype(jnp.float32)

    part_sums = (part_piece(0) + part_piece(1)) + part_piece(2)
    inv_attn = lax.rsqrt(
        jnp.sum(hidden_groups * hidden_groups, axis=(0, 2))[:, None] / D + NORM_EPS
    )
    normed_groups = (
        hidden_groups * inv_attn[None] * attn_gain.reshape(head_count, 1, quarter_width)
    ).astype(jnp.bfloat16)
    compressed = jnp.sum(part_sums, axis=0) * inv_attn
    latent_new = compressed[:, :LATENT]
    latent_new = latent_new * lax.rsqrt(
        jnp.mean(latent_new * latent_new, axis=1, keepdims=True) + NORM_EPS
    )
    new_entry = jnp.concatenate(
        [latent_new, rotate_pairs(compressed[:, LATENT:], cache_lengths)], axis=1
    ).astype(jnp.bfloat16)
    queries = jnp.einsum(
        "gbf,gfq->bq",
        normed_groups,
        w_query.reshape(head_count, quarter_width, w_query.shape[1]),
        preferred_element_type=jnp.float32,
    ).astype(jnp.bfloat16)
    queries = queries.reshape(local_rows, local_heads, NOPE + ROPE)
    absorbed = jnp.einsum(
        "bhn,hnl->bhl", queries[:, :, :NOPE], w_key_up, preferred_element_type=jnp.float32
    ).astype(jnp.bfloat16)
    turned = rotate_pairs(queries[:, :, NOPE:].astype(jnp.float32), cache_lengths).astype(
        jnp.bfloat16
    )
    probes = jnp.concatenate([absorbed, turned], axis=2)
    factor = (NOPE + ROPE) ** (-0.5)
    owner_ids = jnp.arange(peer_count, dtype=jnp.int32)
    dest_owner = request_slot // local_rows
    goes_to = dest_owner[None, :] == owner_ids[:, None]
    sent_any = jnp.max(goes_to.astype(jnp.int32), axis=1)
    sent_row = jnp.sum(jnp.where(goes_to, row_ids[None, :], 0), axis=1)
    sent_slot = request_slot[sent_row]
    sent_len = cache_lengths[sent_row]
    code = jnp.stack(
        [sent_any, sent_slot // 64, sent_slot % 64, sent_len // 64, sent_len % 64], axis=1
    ) * sent_any[:, None]
    code_row = jnp.zeros((peer_count, probes.shape[2]), jnp.float32)
    code_row = code_row.at[:, :5].set(code.astype(jnp.float32)).astype(jnp.bfloat16)
    packed = jnp.concatenate(
        [probes[sent_row], new_entry[sent_row][:, None, :], code_row[:, None, :]], axis=1
    )
    got_packed = lax.all_to_all(packed, "tok", 0, 0, tiled=True)
    got_code = got_packed[:, local_heads + 1, :5].astype(jnp.float32).astype(jnp.int32)
    got_slot = jnp.where(got_code[:, 0] > 0, got_code[:, 1] * 64 + got_code[:, 2], -1)
    got_len = got_code[:, 3] * 64 + got_code[:, 4]
    local_slot = got_slot - tok_index * local_rows
    slot_sel = local_slot[None, :] == row_ids[:, None]
    src_of_slot = jnp.sum(jnp.where(slot_sel, owner_ids[None, :], 0), axis=1)
    owner_probes = got_packed[src_of_slot, :local_heads]
    owner_lengths = got_len[src_of_slot]
    owner_new = got_packed[src_of_slot, local_heads]
    all_heads = lax.all_gather(owner_probes, "head", axis=0, tiled=False)
    numerator, denominator = owner_attend(
        all_heads, owner_lengths, latent_cache, head_index, factor
    )
    joined = head_sum_scatter(jnp.concatenate([numerator, denominator[..., None]], axis=3))
    self_score = factor * jnp.einsum(
        "bhc,bc->bh", owner_probes, owner_new, preferred_element_type=jnp.float32
    )
    self_weight = jnp.exp(self_score).astype(jnp.bfloat16).astype(jnp.float32)
    total_num = joined[:, :, :LATENT] + self_weight[:, :, None] * owner_new[:, None, :LATENT].astype(
        jnp.float32
    )
    total_den = joined[:, :, LATENT] + self_weight
    mixed_latent = (total_num / total_den[:, :, None]).astype(jnp.bfloat16)
    owner_out = jnp.einsum(
        "bhl,hld->bhd", mixed_latent, w_value_up, preferred_element_type=jnp.float32
    ).astype(jnp.bfloat16)
    owner_out = owner_out.reshape(local_rows, local_heads * NOPE)
    owner_out = jnp.concatenate(
        [owner_out, jnp.zeros((1, local_heads * NOPE), jnp.bfloat16)], axis=0
    )
    back_valid = (local_slot >= 0) & (local_slot < local_rows)
    back_row = jnp.where(back_valid, local_slot, local_rows)
    head_out = lax.all_to_all(owner_out[back_row], "tok", 0, 0, tiled=True)[dest_owner]
    head_out = head_out.reshape(local_rows, local_heads * NOPE)
    attn_piece = head_sum_scatter(
        jnp.einsum(
            "bk,kgf->gbf",
            head_out,
            w_out.reshape(w_out.shape[0], head_count, quarter_width),
            preferred_element_type=jnp.float32,
        )
    )
    attended = (hidden.astype(jnp.float32) + attn_piece).astype(jnp.bfloat16)
    attended_wide = attended.astype(jnp.float32)
    expert_count = w_router.shape[1]
    route_count = routes.shape[1]
    expert_ids = jnp.arange(expert_count, dtype=jnp.int32)
    named = routes[:, :, None] == expert_ids[None, None, :]
    struck = jnp.max(named.astype(jnp.int32), axis=1)
    earlier_hits = jnp.cumsum(struck, axis=0) - struck
    capacity = min(local_rows, max(2, 2 * local_rows * route_count // expert_count))
    route_place = routes * capacity + jnp.take_along_axis(earlier_hits, routes, axis=1)
    slot_total = expert_count * capacity
    slot_ids = jnp.arange(slot_total, dtype=jnp.int32)
    filled = route_place[None, :, :] == slot_ids[:, None, None]
    source_token = jnp.sum(
        jnp.where(filled, row_ids[None, :, None], 0), axis=(1, 2)
    ) + local_rows * (1 - jnp.max(filled.astype(jnp.int32), axis=(1, 2)))
    padded_rows = jnp.concatenate(
        [attended, jnp.zeros((1, attended.shape[1]), jnp.bfloat16)], axis=0
    )
    arrived = lax.all_to_all(
        padded_rows[source_token].reshape(expert_count, capacity, quarter_width),
        "tok",
        split_axis=0,
        concat_axis=0,
        tiled=True,
    )
    expert_in = lax.all_to_all(
        jnp.broadcast_to(
            arrived.reshape(1, peer_count * capacity, quarter_width),
            (head_count, peer_count * capacity, quarter_width),
        ),
        "head",
        split_axis=0,
        concat_axis=2,
        tiled=True,
    ).reshape(peer_count * capacity, head_count * quarter_width)
    expert_wide = expert_in.astype(jnp.float32)
    expert_inv = lax.rsqrt(jnp.mean(expert_wide * expert_wide, axis=1, keepdims=True) + NORM_EPS)
    expert_gained = (expert_wide * gain_full).astype(jnp.bfloat16)
    expert_logit = (
        jnp.dot(expert_gained, expert_column, preferred_element_type=jnp.float32)
        * expert_inv[:, 0]
    )
    expert_in = (expert_wide * gain_full * expert_inv).astype(jnp.bfloat16)
    gate_value = jnp.dot(expert_in, expert_gate[0], preferred_element_type=jnp.float32)
    up_value = jnp.dot(expert_in, expert_up[0], preferred_element_type=jnp.float32)
    activity = (jax.nn.silu(gate_value) * up_value).astype(jnp.bfloat16)
    expert_share = head_sum_scatter(
        jnp.einsum(
            "rk,kgf->grf",
            activity,
            expert_down[0].reshape(expert_down.shape[1], head_count, quarter_width),
            preferred_element_type=jnp.float32,
        ).astype(jnp.bfloat16)
    ).astype(jnp.bfloat16)
    logit_hi = lax.reduce_precision(expert_logit, exponent_bits=8, mantissa_bits=7)
    logit_rest = expert_logit - logit_hi
    logit_mid = lax.reduce_precision(logit_rest, exponent_bits=8, mantissa_bits=7)
    logit_lo = logit_rest - logit_mid
    logit_code = jnp.stack([logit_hi, logit_mid, logit_lo], axis=1).reshape(
        peer_count, capacity * 3
    )
    logit_row = jnp.zeros((peer_count, 1, quarter_width), jnp.float32)
    logit_row = logit_row.at[:, 0, : capacity * 3].set(logit_code).astype(jnp.bfloat16)
    returned = lax.all_to_all(
        jnp.concatenate(
            [expert_share.reshape(peer_count, capacity, quarter_width), logit_row], axis=1
        ),
        "tok",
        split_axis=0,
        concat_axis=0,
        tiled=True,
    )
    chosen_rows = returned[:, :capacity].reshape(slot_total, quarter_width)[route_place]
    got_logit = returned[:, capacity, : capacity * 3].reshape(slot_total, 3).astype(jnp.float32)
    slot_logit = (got_logit[:, 0] + got_logit[:, 1]) + got_logit[:, 2]
    picked = slot_logit[route_place]
    lifted = jnp.exp(picked)
    route_weight = lifted / jnp.sum(lifted, axis=1, keepdims=True)
    expert_mix = jnp.sum(route_weight[:, :, None] * chosen_rows.astype(jnp.float32), axis=1).astype(
        jnp.bfloat16
    )
    return (new_entry, attended, expert_mix)


def solution(mesh):
    in_specs = (
        P("tok", "head"),
        P(),
        P(None, "head"),
        P("head", None),
        P("head", None, None),
        P("head", None, None),
        P("head", None),
        P(("tok", "head"), None),
        P("tok"),
        P("tok"),
        P("head"),
        P("head", None),
        P("tok", None),
        P("tok", None, "head"),
        P("tok", None, "head"),
        P("tok", "head", None),
    )
    out_specs = (P("tok", None), P("tok", "head"), P("tok", "head"))
    return jax.shard_map(body, mesh=mesh, in_specs=in_specs, out_specs=out_specs, check_vma=False)
```

```python
import jax
import jax.numpy as jnp
from jax import lax
from jax.sharding import PartitionSpec as P

D = 2048
NOPE = 128
ROPE = 64
LATENT = 512


NORM_EPS = 1e-06


def rotate_pairs(values, places):
    halfway = values.shape[-1] // 2
    freqs = 10000.0 ** (-jnp.arange(halfway, dtype=jnp.float32) / halfway)
    angles = places.astype(jnp.float32).reshape(places.shape + (1,) * (values.ndim - 1)) * freqs
    cosine = jnp.cos(angles)
    sine = jnp.sin(angles)
    first_half = values[..., :halfway]
    second_half = values[..., halfway:]
    return jnp.concatenate(
        [first_half * cosine - second_half * sine, first_half * sine + second_half * cosine],
        axis=-1,
    )


def owner_attend(all_heads, owner_lengths, latent_cache, head_index, factor):
    slot_rows = all_heads.shape[0]
    total_heads = all_heads.shape[1]
    probe_width = all_heads.shape[2]
    key_rows = latent_cache.shape[0]
    starts = jnp.cumsum(owner_lengths) - owner_lengths
    places = head_index * key_rows + jnp.arange(key_rows, dtype=jnp.int32)
    inside = (places[None, :] >= starts[:, None]) & (
        places[None, :] < (starts + owner_lengths)[:, None]
    )
    scores = factor * jnp.einsum(
        "qc,pc->qp",
        all_heads.reshape(slot_rows * total_heads, probe_width),
        latent_cache,
        preferred_element_type=jnp.float32,
    )
    scores = scores.reshape(slot_rows, total_heads, key_rows)
    weights = jnp.where(inside[:, None, :], jnp.exp(scores), 0.0).astype(jnp.bfloat16)
    numerator = jnp.einsum(
        "khp,pl->khl", weights, latent_cache[:, :LATENT], preferred_element_type=jnp.float32
    )
    denominator = jnp.sum(weights.astype(jnp.float32), axis=2)
    return (numerator, denominator)


def head_sum_scatter(values, axis):
    groups = lax.axis_size("head")
    moved = lax.all_to_all(values, "head", split_axis=axis, concat_axis=0, tiled=True)
    moved = moved.reshape((groups, values.shape[0]) + moved.shape[1:])
    return jnp.sum(moved.astype(jnp.float32), axis=0)


def body(
    hidden,
    attn_gain,
    w_query,
    w_latent,
    w_key_up,
    w_value_up,
    w_out,
    latent_cache,
    cache_lengths,
    request_slot,
    ffn_gain,
    w_router,
    routes,
    expert_gate,
    expert_up,
    expert_down,
):
    local_rows = hidden.shape[0]
    quarter_width = hidden.shape[1]
    local_heads = w_key_up.shape[0]
    peer_count = lax.axis_size("tok")
    head_index = lax.axis_index("head")
    tok_index = lax.axis_index("tok")
    row_ids = jnp.arange(local_rows, dtype=jnp.int32)
    latent_width = w_latent.shape[1]
    head_count = lax.axis_size("head")
    gain_part = lax.dynamic_slice_in_dim(attn_gain, head_index * quarter_width, quarter_width, 0)
    raw_part = jnp.dot(
        (hidden.astype(jnp.float32) * gain_part).astype(jnp.bfloat16),
        w_latent,
        preferred_element_type=jnp.float32,
    )
    part_width = -(-latent_width // 128) * 128
    part_hi = lax.reduce_precision(raw_part, exponent_bits=8, mantissa_bits=7)
    rest = raw_part - part_hi
    part_mid = lax.reduce_precision(rest, exponent_bits=8, mantissa_bits=7)
    part_lo = rest - part_mid
    lane_pad = jnp.zeros((local_rows, part_width - latent_width), jnp.bfloat16)
    send_rows = jnp.concatenate(
        [
            hidden,
            part_hi.astype(jnp.bfloat16),
            lane_pad,
            part_mid.astype(jnp.bfloat16),
            lane_pad,
            part_lo.astype(jnp.bfloat16),
            lane_pad,
        ],
        axis=1,
    )
    gain_hi = lax.reduce_precision(ffn_gain, exponent_bits=8, mantissa_bits=7)
    gain_rest = ffn_gain - gain_hi
    gain_mid = lax.reduce_precision(gain_rest, exponent_bits=8, mantissa_bits=7)
    gain_lo = gain_rest - gain_mid
    gain_rows = jnp.zeros((8, send_rows.shape[1]), jnp.bfloat16)
    router_column = lax.dynamic_index_in_dim(w_router, tok_index, axis=1, keepdims=False)
    gain_rows = gain_rows.at[:4, :quarter_width].set(
        jnp.concatenate(
            [jnp.stack([gain_hi, gain_mid, gain_lo]).astype(jnp.bfloat16), router_column[None]],
            axis=0,
        )
    )
    got_all = lax.all_gather(
        jnp.concatenate([send_rows, gain_rows], axis=0), "head", axis=0, tiled=False
    )
    got_rows = got_all[:, :local_rows]
    got_gain = got_all[:, local_rows : local_rows + 3, :quarter_width].astype(jnp.float32)
    gain_full = ((got_gain[:, 0] + got_gain[:, 1]) + got_gain[:, 2]).reshape(-1)
    expert_column = got_all[:, local_rows + 3, :quarter_width].reshape(-1)
    hidden_groups = got_rows[:, :, :quarter_width].astype(jnp.float32)

    def part_piece(k):
        offset = quarter_width + k * part_width
        return got_rows[:, :, offset : offset + latent_width].astype(jnp.float32)

    part_sums = (part_piece(0) + part_piece(1)) + part_piece(2)
    inv_attn = lax.rsqrt(
        jnp.sum(hidden_groups * hidden_groups, axis=(0, 2))[:, None] / D + NORM_EPS
    )
    normed_groups = (
        hidden_groups * inv_attn[None] * attn_gain.reshape(head_count, 1, quarter_width)
    ).astype(jnp.bfloat16)
    compressed = jnp.sum(part_sums, axis=0) * inv_attn
    latent_new = compressed[:, :LATENT]
    latent_new = latent_new * lax.rsqrt(
        jnp.mean(latent_new * latent_new, axis=1, keepdims=True) + NORM_EPS
    )
    new_entry = jnp.concatenate(
        [latent_new, rotate_pairs(compressed[:, LATENT:], cache_lengths)], axis=1
    ).astype(jnp.bfloat16)
    queries = jnp.einsum(
        "gbf,gfq->bq",
        normed_groups,
        w_query.reshape(head_count, quarter_width, w_query.shape[1]),
        preferred_element_type=jnp.float32,
    ).astype(jnp.bfloat16)
    queries = queries.reshape(local_rows, local_heads, NOPE + ROPE)
    absorbed = jnp.einsum(
        "bhn,hnl->bhl", queries[:, :, :NOPE], w_key_up, preferred_element_type=jnp.float32
    ).astype(jnp.bfloat16)
    turned = rotate_pairs(queries[:, :, NOPE:].astype(jnp.float32), cache_lengths).astype(
        jnp.bfloat16
    )
    probes = jnp.concatenate([absorbed, turned], axis=2)
    factor = (NOPE + ROPE) ** (-0.5)
    owner_ids = jnp.arange(peer_count, dtype=jnp.int32)
    dest_owner = request_slot // local_rows
    goes_to = dest_owner[None, :] == owner_ids[:, None]
    sent_any = jnp.max(goes_to.astype(jnp.int32), axis=1)
    sent_row = jnp.sum(jnp.where(goes_to, row_ids[None, :], 0), axis=1)
    sent_slot = request_slot[sent_row]
    sent_len = cache_lengths[sent_row]
    code = jnp.stack(
        [sent_any, sent_slot // 64, sent_slot % 64, sent_len // 64, sent_len % 64], axis=1
    ) * sent_any[:, None]
    code_row = jnp.zeros((peer_count, probes.shape[2]), jnp.float32)
    code_row = code_row.at[:, :5].set(code.astype(jnp.float32)).astype(jnp.bfloat16)
    packed = jnp.concatenate(
        [probes[sent_row], new_entry[sent_row][:, None, :], code_row[:, None, :]], axis=1
    )
    got_packed = lax.all_to_all(packed, "tok", 0, 0, tiled=True)
    got_code = got_packed[:, local_heads + 1, :5].astype(jnp.float32).astype(jnp.int32)
    got_slot = jnp.where(got_code[:, 0] > 0, got_code[:, 1] * 64 + got_code[:, 2], -1)
    got_len = got_code[:, 3] * 64 + got_code[:, 4]
    local_slot = got_slot - tok_index * local_rows
    slot_sel = local_slot[None, :] == row_ids[:, None]
    src_of_slot = jnp.sum(jnp.where(slot_sel, owner_ids[None, :], 0), axis=1)
    owner_probes = got_packed[src_of_slot, :local_heads]
    owner_lengths = got_len[src_of_slot]
    owner_new = got_packed[src_of_slot, local_heads]
    all_heads = lax.all_gather(owner_probes, "head", axis=1, tiled=True)
    numerator, denominator = owner_attend(
        all_heads, owner_lengths, latent_cache, head_index, factor
    )
    joined = head_sum_scatter(jnp.concatenate([numerator, denominator[:, :, None]], axis=2), 1)
    self_score = factor * jnp.einsum(
        "bhc,bc->bh", owner_probes, owner_new, preferred_element_type=jnp.float32
    )
    self_weight = jnp.exp(self_score).astype(jnp.bfloat16).astype(jnp.float32)
    total_num = joined[:, :, :LATENT] + self_weight[:, :, None] * owner_new[:, None, :LATENT].astype(
        jnp.float32
    )
    total_den = joined[:, :, LATENT] + self_weight
    mixed_latent = (total_num / total_den[:, :, None]).astype(jnp.bfloat16)
    owner_out = jnp.einsum(
        "bhl,hld->bhd", mixed_latent, w_value_up, preferred_element_type=jnp.float32
    ).astype(jnp.bfloat16)
    owner_out = owner_out.reshape(local_rows, local_heads * NOPE)
    owner_out = jnp.concatenate(
        [owner_out, jnp.zeros((1, local_heads * NOPE), jnp.bfloat16)], axis=0
    )
    back_valid = (local_slot >= 0) & (local_slot < local_rows)
    back_row = jnp.where(back_valid, local_slot, local_rows)
    head_out = lax.all_to_all(owner_out[back_row], "tok", 0, 0, tiled=True)[dest_owner]
    head_out = head_out.reshape(local_rows, local_heads * NOPE)
    attn_piece = head_sum_scatter(jnp.dot(head_out, w_out, preferred_element_type=jnp.float32), 1)
    attended = (hidden.astype(jnp.float32) + attn_piece).astype(jnp.bfloat16)
    attended_wide = attended.astype(jnp.float32)
    expert_count = w_router.shape[1]
    route_count = routes.shape[1]
    expert_ids = jnp.arange(expert_count, dtype=jnp.int32)
    named = routes[:, :, None] == expert_ids[None, None, :]
    struck = jnp.max(named.astype(jnp.int32), axis=1)
    earlier_hits = jnp.cumsum(struck, axis=0) - struck
    capacity = min(local_rows, max(2, 2 * local_rows * route_count // expert_count))
    route_place = routes * capacity + jnp.take_along_axis(earlier_hits, routes, axis=1)
    slot_total = expert_count * capacity
    slot_ids = jnp.arange(slot_total, dtype=jnp.int32)
    filled = route_place[None, :, :] == slot_ids[:, None, None]
    source_token = jnp.sum(
        jnp.where(filled, row_ids[None, :, None], 0), axis=(1, 2)
    ) + local_rows * (1 - jnp.max(filled.astype(jnp.int32), axis=(1, 2)))
    padded_rows = jnp.concatenate(
        [attended, jnp.zeros((1, attended.shape[1]), jnp.bfloat16)], axis=0
    )
    half = capacity // 2
    source_grid = source_token.reshape(expert_count, capacity)

    def expert_half(lo, hi):
        width = hi - lo
        arrived = lax.all_to_all(
            padded_rows[source_grid[:, lo:hi]], "tok", split_axis=0, concat_axis=0, tiled=True
        )
        expert_in = lax.all_to_all(
            jnp.broadcast_to(
                arrived.reshape(1, peer_count * width, quarter_width),
                (head_count, peer_count * width, quarter_width),
            ),
            "head",
            split_axis=0,
            concat_axis=2,
            tiled=True,
        ).reshape(peer_count * width, head_count * quarter_width)
        expert_wide = expert_in.astype(jnp.float32)
        expert_inv = lax.rsqrt(
            jnp.mean(expert_wide * expert_wide, axis=1, keepdims=True) + NORM_EPS
        )
        expert_gained = (expert_wide * gain_full).astype(jnp.bfloat16)
        expert_logit = (
            jnp.dot(expert_gained, expert_column, preferred_element_type=jnp.float32)
            * expert_inv[:, 0]
        )
        expert_in = (expert_wide * gain_full * expert_inv).astype(jnp.bfloat16)
        gate_value = jnp.dot(expert_in, expert_gate[0], preferred_element_type=jnp.float32)
        up_value = jnp.dot(expert_in, expert_up[0], preferred_element_type=jnp.float32)
        activity = (jax.nn.silu(gate_value) * up_value).astype(jnp.bfloat16)
        share = head_sum_scatter(
            jnp.dot(activity, expert_down[0], preferred_element_type=jnp.float32).astype(
                jnp.bfloat16
            ),
            1,
        ).astype(jnp.bfloat16)
        return share.reshape(peer_count, width, quarter_width), expert_logit.reshape(
            peer_count, width
        )

    share_a, logit_a = expert_half(0, half)
    share_b, logit_b = expert_half(half, capacity)
    expert_share = jnp.concatenate([share_a, share_b], axis=1)
    expert_logit = jnp.concatenate([logit_a, logit_b], axis=1).reshape(-1)
    logit_hi = lax.reduce_precision(expert_logit, exponent_bits=8, mantissa_bits=7)
    logit_rest = expert_logit - logit_hi
    logit_mid = lax.reduce_precision(logit_rest, exponent_bits=8, mantissa_bits=7)
    logit_lo = logit_rest - logit_mid
    logit_code = jnp.stack([logit_hi, logit_mid, logit_lo], axis=1).reshape(
        peer_count, capacity * 3
    )
    logit_row = jnp.zeros((peer_count, 1, quarter_width), jnp.float32)
    logit_row = logit_row.at[:, 0, : capacity * 3].set(logit_code).astype(jnp.bfloat16)
    returned = lax.all_to_all(
        jnp.concatenate(
            [expert_share.reshape(peer_count, capacity, quarter_width), logit_row], axis=1
        ),
        "tok",
        split_axis=0,
        concat_axis=0,
        tiled=True,
    )
    chosen_rows = returned[:, :capacity].reshape(slot_total, quarter_width)[route_place]
    got_logit = returned[:, capacity, : capacity * 3].reshape(slot_total, 3).astype(jnp.float32)
    slot_logit = (got_logit[:, 0] + got_logit[:, 1]) + got_logit[:, 2]
    picked = slot_logit[route_place]
    lifted = jnp.exp(picked)
    route_weight = lifted / jnp.sum(lifted, axis=1, keepdims=True)
    expert_mix = jnp.sum(route_weight[:, :, None] * chosen_rows.astype(jnp.float32), axis=1).astype(
        jnp.bfloat16
    )
    return (new_entry, attended, expert_mix)


def solution(mesh):
    in_specs = (
        P("tok", "head"),
        P(),
        P(None, "head"),
        P("head", None),
        P("head", None, None),
        P("head", None, None),
        P("head", None),
        P(("tok", "head"), None),
        P("tok"),
        P("tok"),
        P("head"),
        P("head", None),
        P("tok", None),
        P("tok", None, "head"),
        P("tok", None, "head"),
        P("tok", "head", None),
    )
    out_specs = (P("tok", None), P("tok", "head"), P("tok", "head"))
    return jax.shard_map(body, mesh=mesh, in_specs=in_specs, out_specs=out_specs, check_vma=False)
```

```python
import jax
import jax.numpy as jnp
from jax import lax
from jax.sharding import PartitionSpec as P

D = 2048
NOPE = 128
ROPE = 64
LATENT = 512


NORM_EPS = 1e-06


def rotate_pairs(values, places):
    halfway = values.shape[-1] // 2
    freqs = 10000.0 ** (-jnp.arange(halfway, dtype=jnp.float32) / halfway)
    angles = places.astype(jnp.float32).reshape(places.shape + (1,) * (values.ndim - 1)) * freqs
    cosine = jnp.cos(angles)
    sine = jnp.sin(angles)
    first_half = values[..., :halfway]
    second_half = values[..., halfway:]
    return jnp.concatenate(
        [first_half * cosine - second_half * sine, first_half * sine + second_half * cosine],
        axis=-1,
    )


def owner_attend(all_heads, owner_lengths, latent_cache, head_index, factor):
    slot_rows = all_heads.shape[0]
    total_heads = all_heads.shape[1]
    probe_width = all_heads.shape[2]
    key_rows = latent_cache.shape[0]
    starts = jnp.cumsum(owner_lengths) - owner_lengths
    places = head_index * key_rows + jnp.arange(key_rows, dtype=jnp.int32)
    inside = (places[None, :] >= starts[:, None]) & (
        places[None, :] < (starts + owner_lengths)[:, None]
    )
    scores = factor * jnp.einsum(
        "qc,pc->qp",
        all_heads.reshape(slot_rows * total_heads, probe_width),
        latent_cache,
        preferred_element_type=jnp.float32,
    )
    scores = scores.reshape(slot_rows, total_heads, key_rows)
    weights = jnp.where(inside[:, None, :], jnp.exp(scores), 0.0).astype(jnp.bfloat16)
    numerator = jnp.einsum(
        "khp,pl->khl", weights, latent_cache[:, :LATENT], preferred_element_type=jnp.float32
    )
    denominator = jnp.sum(weights.astype(jnp.float32), axis=2)
    return (numerator, denominator)


def head_sum_scatter(values, axis):
    groups = lax.axis_size("head")
    moved = lax.all_to_all(values, "head", split_axis=axis, concat_axis=0, tiled=True)
    moved = moved.reshape((groups, values.shape[0]) + moved.shape[1:])
    return jnp.sum(moved.astype(jnp.float32), axis=0)


def body(
    hidden,
    attn_gain,
    w_query,
    w_latent,
    w_key_up,
    w_value_up,
    w_out,
    latent_cache,
    cache_lengths,
    request_slot,
    ffn_gain,
    w_router,
    routes,
    expert_gate,
    expert_up,
    expert_down,
):
    local_rows = hidden.shape[0]
    quarter_width = hidden.shape[1]
    local_heads = w_key_up.shape[0]
    peer_count = lax.axis_size("tok")
    head_index = lax.axis_index("head")
    tok_index = lax.axis_index("tok")
    row_ids = jnp.arange(local_rows, dtype=jnp.int32)
    latent_width = w_latent.shape[1]
    head_count = lax.axis_size("head")
    gain_part = lax.dynamic_slice_in_dim(attn_gain, head_index * quarter_width, quarter_width, 0)
    raw_part = jnp.dot(
        (hidden.astype(jnp.float32) * gain_part).astype(jnp.bfloat16),
        w_latent,
        preferred_element_type=jnp.float32,
    )
    part_width = -(-latent_width // 128) * 128
    part_hi = lax.reduce_precision(raw_part, exponent_bits=8, mantissa_bits=7)
    rest = raw_part - part_hi
    part_mid = lax.reduce_precision(rest, exponent_bits=8, mantissa_bits=7)
    part_lo = rest - part_mid
    lane_pad = jnp.zeros((local_rows, part_width - latent_width), jnp.bfloat16)
    send_rows = jnp.concatenate(
        [
            hidden,
            part_hi.astype(jnp.bfloat16),
            lane_pad,
            part_mid.astype(jnp.bfloat16),
            lane_pad,
            part_lo.astype(jnp.bfloat16),
            lane_pad,
        ],
        axis=1,
    )
    got_rows = lax.all_gather(send_rows, "head", axis=0, tiled=False)
    hidden_groups = got_rows[:, :, :quarter_width].astype(jnp.float32)

    def part_piece(k):
        offset = quarter_width + k * part_width
        return got_rows[:, :, offset : offset + latent_width].astype(jnp.float32)

    part_sums = (part_piece(0) + part_piece(1)) + part_piece(2)
    inv_attn = lax.rsqrt(
        jnp.sum(hidden_groups * hidden_groups, axis=(0, 2))[:, None] / D + NORM_EPS
    )
    normed_groups = (
        hidden_groups * inv_attn[None] * attn_gain.reshape(head_count, 1, quarter_width)
    ).astype(jnp.bfloat16)
    compressed = jnp.sum(part_sums, axis=0) * inv_attn
    latent_new = compressed[:, :LATENT]
    latent_new = latent_new * lax.rsqrt(
        jnp.mean(latent_new * latent_new, axis=1, keepdims=True) + NORM_EPS
    )
    new_entry = jnp.concatenate(
        [latent_new, rotate_pairs(compressed[:, LATENT:], cache_lengths)], axis=1
    ).astype(jnp.bfloat16)
    queries = jnp.einsum(
        "gbf,gfq->bq",
        normed_groups,
        w_query.reshape(head_count, quarter_width, w_query.shape[1]),
        preferred_element_type=jnp.float32,
    ).astype(jnp.bfloat16)
    queries = queries.reshape(local_rows, local_heads, NOPE + ROPE)
    absorbed = jnp.einsum(
        "bhn,hnl->bhl", queries[:, :, :NOPE], w_key_up, preferred_element_type=jnp.float32
    ).astype(jnp.bfloat16)
    turned = rotate_pairs(queries[:, :, NOPE:].astype(jnp.float32), cache_lengths).astype(
        jnp.bfloat16
    )
    probes = jnp.concatenate([absorbed, turned], axis=2)
    factor = (NOPE + ROPE) ** (-0.5)
    owner_ids = jnp.arange(peer_count, dtype=jnp.int32)
    dest_owner = request_slot // local_rows
    goes_to = dest_owner[None, :] == owner_ids[:, None]
    sent_any = jnp.max(goes_to.astype(jnp.int32), axis=1)
    sent_row = jnp.sum(jnp.where(goes_to, row_ids[None, :], 0), axis=1)
    sent_slot = request_slot[sent_row]
    sent_len = cache_lengths[sent_row]
    code = jnp.stack(
        [sent_any, sent_slot // 64, sent_slot % 64, sent_len // 64, sent_len % 64], axis=1
    ) * sent_any[:, None]
    code_row = jnp.zeros((peer_count, probes.shape[2]), jnp.float32)
    code_row = code_row.at[:, :5].set(code.astype(jnp.float32)).astype(jnp.bfloat16)
    packed = jnp.concatenate(
        [probes[sent_row], new_entry[sent_row][:, None, :], code_row[:, None, :]], axis=1
    )
    got_packed = lax.all_to_all(packed, "tok", 0, 0, tiled=True)
    got_code = got_packed[:, local_heads + 1, :5].astype(jnp.float32).astype(jnp.int32)
    got_slot = jnp.where(got_code[:, 0] > 0, got_code[:, 1] * 64 + got_code[:, 2], -1)
    got_len = got_code[:, 3] * 64 + got_code[:, 4]
    local_slot = got_slot - tok_index * local_rows
    slot_sel = local_slot[None, :] == row_ids[:, None]
    src_of_slot = jnp.sum(jnp.where(slot_sel, owner_ids[None, :], 0), axis=1)
    owner_probes = got_packed[src_of_slot, :local_heads]
    owner_lengths = got_len[src_of_slot]
    owner_new = got_packed[src_of_slot, local_heads]
    all_heads = lax.all_gather(owner_probes, "head", axis=1, tiled=True)
    numerator, denominator = owner_attend(
        all_heads, owner_lengths, latent_cache, head_index, factor
    )
    joined = head_sum_scatter(jnp.concatenate([numerator, denominator[:, :, None]], axis=2), 1)
    self_score = factor * jnp.einsum(
        "bhc,bc->bh", owner_probes, owner_new, preferred_element_type=jnp.float32
    )
    self_weight = jnp.exp(self_score).astype(jnp.bfloat16).astype(jnp.float32)
    total_num = joined[:, :, :LATENT] + self_weight[:, :, None] * owner_new[:, None, :LATENT].astype(
        jnp.float32
    )
    total_den = joined[:, :, LATENT] + self_weight
    mixed_latent = (total_num / total_den[:, :, None]).astype(jnp.bfloat16)
    owner_out = jnp.einsum(
        "bhl,hld->bhd", mixed_latent, w_value_up, preferred_element_type=jnp.float32
    ).astype(jnp.bfloat16)
    owner_out = owner_out.reshape(local_rows, local_heads * NOPE)
    owner_out = jnp.concatenate(
        [owner_out, jnp.zeros((1, local_heads * NOPE), jnp.bfloat16)], axis=0
    )
    back_valid = (local_slot >= 0) & (local_slot < local_rows)
    back_row = jnp.where(back_valid, local_slot, local_rows)
    head_out = lax.all_to_all(owner_out[back_row], "tok", 0, 0, tiled=True)[dest_owner]
    head_out = head_out.reshape(local_rows, local_heads * NOPE)
    attn_piece = head_sum_scatter(jnp.dot(head_out, w_out, preferred_element_type=jnp.float32), 1)
    attended = (hidden.astype(jnp.float32) + attn_piece).astype(jnp.bfloat16)
    attended_wide = attended.astype(jnp.float32)
    gained = (attended_wide * ffn_gain).astype(jnp.bfloat16)
    squares, logit_part = lax.psum(
        (
            jnp.sum(attended_wide * attended_wide, axis=1),
            jnp.dot(gained, w_router, preferred_element_type=jnp.float32),
        ),
        "head",
    )
    inv_ffn = lax.rsqrt(squares / D + NORM_EPS)
    logits = logit_part * inv_ffn[:, None]
    normed_ffn = (attended_wide * ffn_gain * inv_ffn[:, None]).astype(jnp.bfloat16)
    expert_count = w_router.shape[1]
    route_count = routes.shape[1]
    expert_ids = jnp.arange(expert_count, dtype=jnp.int32)
    named = routes[:, :, None] == expert_ids[None, None, :]
    picked = jnp.sum(jnp.where(named, logits[:, None, :], 0.0), axis=2)
    lifted = jnp.exp(picked)
    route_weight = lifted / jnp.sum(lifted, axis=1, keepdims=True)
    struck = jnp.max(named.astype(jnp.int32), axis=1)
    earlier_hits = jnp.cumsum(struck, axis=0) - struck
    capacity = min(local_rows, max(2, 2 * local_rows * route_count // expert_count))
    route_place = routes * capacity + jnp.take_along_axis(earlier_hits, routes, axis=1)
    slot_total = expert_count * capacity
    slot_ids = jnp.arange(slot_total, dtype=jnp.int32)
    filled = route_place[None, :, :] == slot_ids[:, None, None]
    source_token = jnp.sum(
        jnp.where(filled, row_ids[None, :, None], 0), axis=(1, 2)
    ) + local_rows * (1 - jnp.max(filled.astype(jnp.int32), axis=(1, 2)))
    padded_rows = jnp.concatenate(
        [normed_ffn, jnp.zeros((1, normed_ffn.shape[1]), jnp.bfloat16)], axis=0
    )
    arrived = lax.all_to_all(
        padded_rows[source_token].reshape(expert_count, capacity, quarter_width),
        "tok",
        split_axis=0,
        concat_axis=0,
        tiled=True,
    )
    expert_in = lax.all_gather(
        arrived.reshape(peer_count * capacity, quarter_width), "head", axis=1, tiled=True
    )
    gate_value = jnp.dot(expert_in, expert_gate[0], preferred_element_type=jnp.float32)
    up_value = jnp.dot(expert_in, expert_up[0], preferred_element_type=jnp.float32)
    activity = (jax.nn.silu(gate_value) * up_value).astype(jnp.bfloat16)
    expert_share = head_sum_scatter(
        jnp.dot(activity, expert_down[0], preferred_element_type=jnp.float32).astype(jnp.bfloat16),
        1,
    ).astype(jnp.bfloat16)
    returned = lax.all_to_all(
        expert_share.reshape(peer_count, capacity, quarter_width),
        "tok",
        split_axis=0,
        concat_axis=0,
        tiled=True,
    )
    chosen_rows = returned.reshape(slot_total, quarter_width)[route_place]
    expert_mix = jnp.sum(route_weight[:, :, None] * chosen_rows.astype(jnp.float32), axis=1).astype(
        jnp.bfloat16
    )
    return (new_entry, attended, expert_mix)


def solution(mesh):
    in_specs = (
        P("tok", "head"),
        P(),
        P(None, "head"),
        P("head", None),
        P("head", None, None),
        P("head", None, None),
        P("head", None),
        P(("tok", "head"), None),
        P("tok"),
        P("tok"),
        P("head"),
        P("head", None),
        P("tok", None),
        P("tok", None, "head"),
        P("tok", None, "head"),
        P("tok", "head", None),
    )
    out_specs = (P("tok", None), P("tok", "head"), P("tok", "head"))
    return jax.shard_map(body, mesh=mesh, in_specs=in_specs, out_specs=out_specs, check_vma=False)
```

```python
import jax
import jax.numpy as jnp
from jax import lax
from jax.sharding import PartitionSpec as P

D = 2048
NOPE = 128
ROPE = 64
LATENT = 512


NORM_EPS = 1e-06


def rotate_pairs(values, places):
    halfway = values.shape[-1] // 2
    freqs = 10000.0 ** (-jnp.arange(halfway, dtype=jnp.float32) / halfway)
    angles = places.astype(jnp.float32).reshape(places.shape + (1,) * (values.ndim - 1)) * freqs
    cosine = jnp.cos(angles)
    sine = jnp.sin(angles)
    first_half = values[..., :halfway]
    second_half = values[..., halfway:]
    return jnp.concatenate(
        [first_half * cosine - second_half * sine, first_half * sine + second_half * cosine],
        axis=-1,
    )


def owner_attend(all_heads, owner_lengths, latent_cache, head_index, factor):
    slot_rows = all_heads.shape[0]
    total_heads = all_heads.shape[1]
    probe_width = all_heads.shape[2]
    key_rows = latent_cache.shape[0]
    starts = jnp.cumsum(owner_lengths) - owner_lengths
    places = head_index * key_rows + jnp.arange(key_rows, dtype=jnp.int32)
    inside = (places[None, :] >= starts[:, None]) & (
        places[None, :] < (starts + owner_lengths)[:, None]
    )
    scores = factor * jnp.einsum(
        "qc,pc->qp",
        all_heads.reshape(slot_rows * total_heads, probe_width),
        latent_cache,
        preferred_element_type=jnp.float32,
    )
    scores = scores.reshape(slot_rows, total_heads, key_rows)
    weights = jnp.where(inside[:, None, :], jnp.exp(scores), 0.0).astype(jnp.bfloat16)
    numerator = jnp.einsum(
        "khp,pl->khl", weights, latent_cache[:, :LATENT], preferred_element_type=jnp.float32
    )
    denominator = jnp.sum(weights.astype(jnp.float32), axis=2)
    return (numerator, denominator)


def head_sum_scatter(values, axis):
    groups = lax.axis_size("head")
    moved = lax.all_to_all(values, "head", split_axis=axis, concat_axis=0, tiled=True)
    moved = moved.reshape((groups, values.shape[0]) + moved.shape[1:])
    return jnp.sum(moved.astype(jnp.float32), axis=0)


def body(
    hidden,
    attn_gain,
    w_query,
    w_latent,
    w_key_up,
    w_value_up,
    w_out,
    latent_cache,
    cache_lengths,
    request_slot,
    ffn_gain,
    w_router,
    routes,
    expert_gate,
    expert_up,
    expert_down,
):
    local_rows = hidden.shape[0]
    quarter_width = hidden.shape[1]
    local_heads = w_key_up.shape[0]
    peer_count = lax.axis_size("tok")
    head_index = lax.axis_index("head")
    tok_index = lax.axis_index("tok")
    row_ids = jnp.arange(local_rows, dtype=jnp.int32)
    latent_width = w_latent.shape[1]
    head_count = lax.axis_size("head")
    gain_part = lax.dynamic_slice_in_dim(attn_gain, head_index * quarter_width, quarter_width, 0)
    raw_part = jnp.dot(
        (hidden.astype(jnp.float32) * gain_part).astype(jnp.bfloat16),
        w_latent,
        preferred_element_type=jnp.float32,
    )
    part_width = -(-latent_width // 128) * 128
    part_hi = lax.reduce_precision(raw_part, exponent_bits=8, mantissa_bits=7)
    rest = raw_part - part_hi
    part_mid = lax.reduce_precision(rest, exponent_bits=8, mantissa_bits=7)
    part_lo = rest - part_mid
    lane_pad = jnp.zeros((local_rows, part_width - latent_width), jnp.bfloat16)
    send_rows = jnp.concatenate(
        [
            hidden,
            part_hi.astype(jnp.bfloat16),
            lane_pad,
            part_mid.astype(jnp.bfloat16),
            lane_pad,
            part_lo.astype(jnp.bfloat16),
            lane_pad,
        ],
        axis=1,
    )
    got_rows = lax.all_gather(send_rows, "head", axis=0, tiled=False)
    hidden_groups = got_rows[:, :, :quarter_width].astype(jnp.float32)

    def part_piece(k):
        offset = quarter_width + k * part_width
        return got_rows[:, :, offset : offset + latent_width].astype(jnp.float32)

    part_sums = (part_piece(0) + part_piece(1)) + part_piece(2)
    inv_attn = lax.rsqrt(
        jnp.sum(hidden_groups * hidden_groups, axis=(0, 2))[:, None] / D + NORM_EPS
    )
    normed_groups = (
        hidden_groups * inv_attn[None] * attn_gain.reshape(head_count, 1, quarter_width)
    ).astype(jnp.bfloat16)
    compressed = jnp.sum(part_sums, axis=0) * inv_attn
    latent_new = compressed[:, :LATENT]
    latent_new = latent_new * lax.rsqrt(
        jnp.mean(latent_new * latent_new, axis=1, keepdims=True) + NORM_EPS
    )
    new_entry = jnp.concatenate(
        [latent_new, rotate_pairs(compressed[:, LATENT:], cache_lengths)], axis=1
    ).astype(jnp.bfloat16)
    queries = jnp.einsum(
        "gbf,gfq->bq",
        normed_groups,
        w_query.reshape(head_count, quarter_width, w_query.shape[1]),
        preferred_element_type=jnp.float32,
    ).astype(jnp.bfloat16)
    queries = queries.reshape(local_rows, local_heads, NOPE + ROPE)
    absorbed = jnp.einsum(
        "bhn,hnl->bhl", queries[:, :, :NOPE], w_key_up, preferred_element_type=jnp.float32
    ).astype(jnp.bfloat16)
    turned = rotate_pairs(queries[:, :, NOPE:].astype(jnp.float32), cache_lengths).astype(
        jnp.bfloat16
    )
    probes = jnp.concatenate([absorbed, turned], axis=2)
    factor = (NOPE + ROPE) ** (-0.5)
    owner_ids = jnp.arange(peer_count, dtype=jnp.int32)
    dest_owner = request_slot // local_rows
    goes_to = dest_owner[None, :] == owner_ids[:, None]
    sent_any = jnp.max(goes_to.astype(jnp.int32), axis=1)
    sent_row = jnp.sum(jnp.where(goes_to, row_ids[None, :], 0), axis=1)
    sent_slot = request_slot[sent_row]
    sent_len = cache_lengths[sent_row]
    code = jnp.stack(
        [sent_any, sent_slot // 64, sent_slot % 64, sent_len // 64, sent_len % 64], axis=1
    ) * sent_any[:, None]
    code_row = jnp.zeros((peer_count, probes.shape[2]), jnp.float32)
    code_row = code_row.at[:, :5].set(code.astype(jnp.float32)).astype(jnp.bfloat16)
    packed = jnp.concatenate(
        [probes[sent_row], new_entry[sent_row][:, None, :], code_row[:, None, :]], axis=1
    )
    got_packed = lax.all_to_all(packed, "tok", 0, 0, tiled=True)
    got_code = got_packed[:, local_heads + 1, :5].astype(jnp.float32).astype(jnp.int32)
    got_slot = jnp.where(got_code[:, 0] > 0, got_code[:, 1] * 64 + got_code[:, 2], -1)
    got_len = got_code[:, 3] * 64 + got_code[:, 4]
    local_slot = got_slot - tok_index * local_rows
    slot_sel = local_slot[None, :] == row_ids[:, None]
    src_of_slot = jnp.sum(jnp.where(slot_sel, owner_ids[None, :], 0), axis=1)
    owner_probes = got_packed[src_of_slot, :local_heads]
    owner_lengths = got_len[src_of_slot]
    owner_new = got_packed[src_of_slot, local_heads]
    all_heads = lax.all_gather(owner_probes, "head", axis=1, tiled=True)
    numerator, denominator = owner_attend(
        all_heads, owner_lengths, latent_cache, head_index, factor
    )
    den_row = jnp.zeros((1, denominator.shape[1], LATENT), jnp.float32)
    den_row = den_row.at[0, :, : denominator.shape[0]].set(denominator.T)
    joined = head_sum_scatter(jnp.concatenate([numerator, den_row], axis=0), 1)
    group_den = joined[local_rows, :, :local_rows].T
    self_score = factor * jnp.einsum(
        "bhc,bc->bh", owner_probes, owner_new, preferred_element_type=jnp.float32
    )
    self_weight = jnp.exp(self_score).astype(jnp.bfloat16).astype(jnp.float32)
    total_num = joined[:local_rows] + self_weight[:, :, None] * owner_new[:, None, :LATENT].astype(
        jnp.float32
    )
    total_den = group_den + self_weight
    mixed_latent = (total_num / total_den[:, :, None]).astype(jnp.bfloat16)
    owner_out = jnp.einsum(
        "bhl,hld->bhd", mixed_latent, w_value_up, preferred_element_type=jnp.float32
    ).astype(jnp.bfloat16)
    owner_out = owner_out.reshape(local_rows, local_heads * NOPE)
    owner_out = jnp.concatenate(
        [owner_out, jnp.zeros((1, local_heads * NOPE), jnp.bfloat16)], axis=0
    )
    back_valid = (local_slot >= 0) & (local_slot < local_rows)
    back_row = jnp.where(back_valid, local_slot, local_rows)
    head_out = lax.all_to_all(owner_out[back_row], "tok", 0, 0, tiled=True)[dest_owner]
    head_out = head_out.reshape(local_rows, local_heads * NOPE)
    attn_piece = head_sum_scatter(jnp.dot(head_out, w_out, preferred_element_type=jnp.float32), 1)
    attended = (hidden.astype(jnp.float32) + attn_piece).astype(jnp.bfloat16)
    attended_wide = attended.astype(jnp.float32)
    gained = (attended_wide * ffn_gain).astype(jnp.bfloat16)
    squares, logit_part = lax.psum(
        (
            jnp.sum(attended_wide * attended_wide, axis=1),
            jnp.dot(gained, w_router, preferred_element_type=jnp.float32),
        ),
        "head",
    )
    inv_ffn = lax.rsqrt(squares / D + NORM_EPS)
    logits = logit_part * inv_ffn[:, None]
    normed_ffn = (attended_wide * ffn_gain * inv_ffn[:, None]).astype(jnp.bfloat16)
    expert_count = w_router.shape[1]
    route_count = routes.shape[1]
    expert_ids = jnp.arange(expert_count, dtype=jnp.int32)
    named = routes[:, :, None] == expert_ids[None, None, :]
    picked = jnp.sum(jnp.where(named, logits[:, None, :], 0.0), axis=2)
    lifted = jnp.exp(picked)
    route_weight = lifted / jnp.sum(lifted, axis=1, keepdims=True)
    struck = jnp.max(named.astype(jnp.int32), axis=1)
    earlier_hits = jnp.cumsum(struck, axis=0) - struck
    capacity = min(local_rows, max(2, 2 * local_rows * route_count // expert_count))
    route_place = routes * capacity + jnp.take_along_axis(earlier_hits, routes, axis=1)
    slot_total = expert_count * capacity
    slot_ids = jnp.arange(slot_total, dtype=jnp.int32)
    filled = route_place[None, :, :] == slot_ids[:, None, None]
    source_token = jnp.sum(
        jnp.where(filled, row_ids[None, :, None], 0), axis=(1, 2)
    ) + local_rows * (1 - jnp.max(filled.astype(jnp.int32), axis=(1, 2)))
    padded_rows = jnp.concatenate(
        [normed_ffn, jnp.zeros((1, normed_ffn.shape[1]), jnp.bfloat16)], axis=0
    )
    arrived = lax.all_to_all(
        padded_rows[source_token].reshape(expert_count, capacity, quarter_width),
        "tok",
        split_axis=0,
        concat_axis=0,
        tiled=True,
    )
    expert_in = lax.all_to_all(
        jnp.broadcast_to(
            arrived.reshape(1, peer_count * capacity, quarter_width),
            (head_count, peer_count * capacity, quarter_width),
        ),
        "head",
        split_axis=0,
        concat_axis=2,
        tiled=True,
    ).reshape(peer_count * capacity, head_count * quarter_width)
    gate_value = jnp.dot(expert_in, expert_gate[0], preferred_element_type=jnp.float32)
    up_value = jnp.dot(expert_in, expert_up[0], preferred_element_type=jnp.float32)
    activity = (jax.nn.silu(gate_value) * up_value).astype(jnp.bfloat16)
    expert_share = head_sum_scatter(
        jnp.dot(activity, expert_down[0], preferred_element_type=jnp.float32).astype(jnp.bfloat16),
        1,
    ).astype(jnp.bfloat16)
    returned = lax.all_to_all(
        expert_share.reshape(peer_count, capacity, quarter_width),
        "tok",
        split_axis=0,
        concat_axis=0,
        tiled=True,
    )
    chosen_rows = returned.reshape(slot_total, quarter_width)[route_place]
    expert_mix = jnp.sum(route_weight[:, :, None] * chosen_rows.astype(jnp.float32), axis=1).astype(
        jnp.bfloat16
    )
    return (new_entry, attended, expert_mix)


def solution(mesh):
    in_specs = (
        P("tok", "head"),
        P(),
        P(None, "head"),
        P("head", None),
        P("head", None, None),
        P("head", None, None),
        P("head", None),
        P(("tok", "head"), None),
        P("tok"),
        P("tok"),
        P("head"),
        P("head", None),
        P("tok", None),
        P("tok", None, "head"),
        P("tok", None, "head"),
        P("tok", "head", None),
    )
    out_specs = (P("tok", None), P("tok", "head"), P("tok", "head"))
    return jax.shard_map(body, mesh=mesh, in_specs=in_specs, out_specs=out_specs, check_vma=False)
```

```python
import jax
import jax.numpy as jnp
from jax import lax
from jax.sharding import PartitionSpec as P

D = 2048
NOPE = 128
ROPE = 64
LATENT = 512


NORM_EPS = 1e-06


def rotate_pairs(values, places):
    halfway = values.shape[-1] // 2
    freqs = 10000.0 ** (-jnp.arange(halfway, dtype=jnp.float32) / halfway)
    angles = places.astype(jnp.float32).reshape(places.shape + (1,) * (values.ndim - 1)) * freqs
    cosine = jnp.cos(angles)
    sine = jnp.sin(angles)
    first_half = values[..., :halfway]
    second_half = values[..., halfway:]
    return jnp.concatenate(
        [first_half * cosine - second_half * sine, first_half * sine + second_half * cosine],
        axis=-1,
    )


def owner_attend(all_heads, owner_lengths, latent_cache, head_index, factor):
    slot_rows = all_heads.shape[0]
    total_heads = all_heads.shape[1]
    probe_width = all_heads.shape[2]
    key_rows = latent_cache.shape[0]
    starts = jnp.cumsum(owner_lengths) - owner_lengths
    places = head_index * key_rows + jnp.arange(key_rows, dtype=jnp.int32)
    inside = (places[None, :] >= starts[:, None]) & (
        places[None, :] < (starts + owner_lengths)[:, None]
    )
    scores = factor * jnp.einsum(
        "qc,pc->qp",
        all_heads.reshape(slot_rows * total_heads, probe_width),
        latent_cache,
        preferred_element_type=jnp.float32,
    )
    scores = scores.reshape(slot_rows, total_heads, key_rows)
    weights = jnp.where(inside[:, None, :], jnp.exp(scores), 0.0).astype(jnp.bfloat16)
    numerator = jnp.einsum(
        "khp,pl->khl", weights, latent_cache[:, :LATENT], preferred_element_type=jnp.float32
    )
    denominator = jnp.sum(weights.astype(jnp.float32), axis=2)
    return (numerator, denominator)


def head_sum_scatter(values, axis):
    groups = lax.axis_size("head")
    moved = lax.all_to_all(values, "head", split_axis=axis, concat_axis=0, tiled=True)
    moved = moved.reshape((groups, values.shape[0]) + moved.shape[1:])
    return jnp.sum(moved.astype(jnp.float32), axis=0)


def body(
    hidden,
    attn_gain,
    w_query,
    w_latent,
    w_key_up,
    w_value_up,
    w_out,
    latent_cache,
    cache_lengths,
    request_slot,
    ffn_gain,
    w_router,
    routes,
    expert_gate,
    expert_up,
    expert_down,
):
    local_rows = hidden.shape[0]
    quarter_width = hidden.shape[1]
    local_heads = w_key_up.shape[0]
    peer_count = lax.axis_size("tok")
    head_index = lax.axis_index("head")
    tok_index = lax.axis_index("tok")
    row_ids = jnp.arange(local_rows, dtype=jnp.int32)
    latent_width = w_latent.shape[1]
    head_count = lax.axis_size("head")
    gain_part = lax.dynamic_slice_in_dim(attn_gain, head_index * quarter_width, quarter_width, 0)
    raw_part = jnp.dot(
        (hidden.astype(jnp.float32) * gain_part).astype(jnp.bfloat16),
        w_latent,
        preferred_element_type=jnp.float32,
    )
    part_width = -(-latent_width // 128) * 128
    part_hi = lax.reduce_precision(raw_part, exponent_bits=8, mantissa_bits=7)
    rest = raw_part - part_hi
    part_mid = lax.reduce_precision(rest, exponent_bits=8, mantissa_bits=7)
    part_lo = rest - part_mid
    lane_pad = jnp.zeros((local_rows, part_width - latent_width), jnp.bfloat16)
    send_rows = jnp.concatenate(
        [
            hidden,
            part_hi.astype(jnp.bfloat16),
            lane_pad,
            part_mid.astype(jnp.bfloat16),
            lane_pad,
            part_lo.astype(jnp.bfloat16),
            lane_pad,
        ],
        axis=1,
    )
    got_rows = lax.all_gather(send_rows, "head", axis=0, tiled=False)
    hidden_groups = got_rows[:, :, :quarter_width].astype(jnp.float32)

    def part_piece(k):
        offset = quarter_width + k * part_width
        return got_rows[:, :, offset : offset + latent_width].astype(jnp.float32)

    part_sums = (part_piece(0) + part_piece(1)) + part_piece(2)
    inv_attn = lax.rsqrt(
        jnp.sum(hidden_groups * hidden_groups, axis=(0, 2))[:, None] / D + NORM_EPS
    )
    normed_groups = (
        hidden_groups * inv_attn[None] * attn_gain.reshape(head_count, 1, quarter_width)
    ).astype(jnp.bfloat16)
    compressed = jnp.sum(part_sums, axis=0) * inv_attn
    latent_new = compressed[:, :LATENT]
    latent_new = latent_new * lax.rsqrt(
        jnp.mean(latent_new * latent_new, axis=1, keepdims=True) + NORM_EPS
    )
    new_entry = jnp.concatenate(
        [latent_new, rotate_pairs(compressed[:, LATENT:], cache_lengths)], axis=1
    ).astype(jnp.bfloat16)
    queries = jnp.einsum(
        "gbf,gfq->bq",
        normed_groups,
        w_query.reshape(head_count, quarter_width, w_query.shape[1]),
        preferred_element_type=jnp.float32,
    ).astype(jnp.bfloat16)
    queries = queries.reshape(local_rows, local_heads, NOPE + ROPE)
    absorbed = jnp.einsum(
        "bhn,hnl->bhl", queries[:, :, :NOPE], w_key_up, preferred_element_type=jnp.float32
    ).astype(jnp.bfloat16)
    turned = rotate_pairs(queries[:, :, NOPE:].astype(jnp.float32), cache_lengths).astype(
        jnp.bfloat16
    )
    probes = jnp.concatenate([absorbed, turned], axis=2)
    factor = (NOPE + ROPE) ** (-0.5)
    owner_ids = jnp.arange(peer_count, dtype=jnp.int32)
    dest_owner = request_slot // local_rows
    goes_to = dest_owner[None, :] == owner_ids[:, None]
    sent_any = jnp.max(goes_to.astype(jnp.int32), axis=1)
    sent_row = jnp.sum(jnp.where(goes_to, row_ids[None, :], 0), axis=1)
    sent_slot = request_slot[sent_row]
    sent_len = cache_lengths[sent_row]
    code = jnp.stack(
        [sent_any, sent_slot // 64, sent_slot % 64, sent_len // 64, sent_len % 64], axis=1
    ) * sent_any[:, None]
    code_row = jnp.zeros((peer_count, probes.shape[2]), jnp.float32)
    code_row = code_row.at[:, :5].set(code.astype(jnp.float32)).astype(jnp.bfloat16)
    packed = jnp.concatenate(
        [probes[sent_row], new_entry[sent_row][:, None, :], code_row[:, None, :]], axis=1
    )
    got_packed = lax.all_to_all(packed, "tok", 0, 0, tiled=True)
    got_code = got_packed[:, local_heads + 1, :5].astype(jnp.float32).astype(jnp.int32)
    got_slot = jnp.where(got_code[:, 0] > 0, got_code[:, 1] * 64 + got_code[:, 2], -1)
    got_len = got_code[:, 3] * 64 + got_code[:, 4]
    local_slot = got_slot - tok_index * local_rows
    slot_sel = local_slot[None, :] == row_ids[:, None]
    src_of_slot = jnp.sum(jnp.where(slot_sel, owner_ids[None, :], 0), axis=1)
    owner_probes = got_packed[src_of_slot, :local_heads]
    owner_lengths = got_len[src_of_slot]
    owner_new = got_packed[src_of_slot, local_heads]
    all_heads = lax.all_gather(owner_probes, "head", axis=1, tiled=True)
    numerator, denominator = owner_attend(
        all_heads, owner_lengths, latent_cache, head_index, factor
    )
    den_row = jnp.zeros((1, denominator.shape[1], LATENT), jnp.float32)
    den_row = den_row.at[0, :, : denominator.shape[0]].set(denominator.T)
    joined = head_sum_scatter(jnp.concatenate([numerator, den_row], axis=0), 1)
    group_den = joined[local_rows, :, :local_rows].T
    self_score = factor * jnp.einsum(
        "bhc,bc->bh", owner_probes, owner_new, preferred_element_type=jnp.float32
    )
    self_weight = jnp.exp(self_score).astype(jnp.bfloat16).astype(jnp.float32)
    total_num = joined[:local_rows] + self_weight[:, :, None] * owner_new[:, None, :LATENT].astype(
        jnp.float32
    )
    total_den = group_den + self_weight
    mixed_latent = (total_num / total_den[:, :, None]).astype(jnp.bfloat16)
    owner_out = jnp.einsum(
        "bhl,hld->bhd", mixed_latent, w_value_up, preferred_element_type=jnp.float32
    ).astype(jnp.bfloat16)
    owner_out = owner_out.reshape(local_rows, local_heads * NOPE)
    owner_out = jnp.concatenate(
        [owner_out, jnp.zeros((1, local_heads * NOPE), jnp.bfloat16)], axis=0
    )
    back_valid = (local_slot >= 0) & (local_slot < local_rows)
    back_row = jnp.where(back_valid, local_slot, local_rows)
    head_out = lax.all_to_all(owner_out[back_row], "tok", 0, 0, tiled=True)[dest_owner]
    head_out = head_out.reshape(local_rows, local_heads * NOPE)
    attn_piece = head_sum_scatter(jnp.dot(head_out, w_out, preferred_element_type=jnp.float32), 1)
    attended = (hidden.astype(jnp.float32) + attn_piece).astype(jnp.bfloat16)
    attended_wide = attended.astype(jnp.float32)
    gained = (attended_wide * ffn_gain).astype(jnp.bfloat16)
    squares, logit_part = lax.psum(
        (
            jnp.sum(attended_wide * attended_wide, axis=1),
            jnp.dot(gained, w_router, preferred_element_type=jnp.float32),
        ),
        "head",
    )
    inv_ffn = lax.rsqrt(squares / D + NORM_EPS)
    logits = logit_part * inv_ffn[:, None]
    normed_ffn = (attended_wide * ffn_gain * inv_ffn[:, None]).astype(jnp.bfloat16)
    expert_count = w_router.shape[1]
    route_count = routes.shape[1]
    expert_ids = jnp.arange(expert_count, dtype=jnp.int32)
    named = routes[:, :, None] == expert_ids[None, None, :]
    picked = jnp.sum(jnp.where(named, logits[:, None, :], 0.0), axis=2)
    lifted = jnp.exp(picked)
    route_weight = lifted / jnp.sum(lifted, axis=1, keepdims=True)
    struck = jnp.max(named.astype(jnp.int32), axis=1)
    earlier_hits = jnp.cumsum(struck, axis=0) - struck
    capacity = min(local_rows, max(2, 2 * local_rows * route_count // expert_count))
    route_place = routes * capacity + jnp.take_along_axis(earlier_hits, routes, axis=1)
    slot_total = expert_count * capacity
    slot_ids = jnp.arange(slot_total, dtype=jnp.int32)
    filled = route_place[None, :, :] == slot_ids[:, None, None]
    source_token = jnp.sum(
        jnp.where(filled, row_ids[None, :, None], 0), axis=(1, 2)
    ) + local_rows * (1 - jnp.max(filled.astype(jnp.int32), axis=(1, 2)))
    padded_rows = jnp.concatenate(
        [normed_ffn, jnp.zeros((1, normed_ffn.shape[1]), jnp.bfloat16)], axis=0
    )
    arrived = lax.all_to_all(
        padded_rows[source_token].reshape(expert_count, capacity * quarter_width),
        "tok",
        split_axis=0,
        concat_axis=0,
        tiled=True,
    )
    expert_in = lax.all_to_all(
        jnp.broadcast_to(
            arrived.reshape(1, peer_count * capacity, quarter_width),
            (head_count, peer_count * capacity, quarter_width),
        ),
        "head",
        split_axis=0,
        concat_axis=2,
        tiled=True,
    ).reshape(peer_count * capacity, head_count * quarter_width)
    gate_value = jnp.dot(expert_in, expert_gate[0], preferred_element_type=jnp.float32)
    up_value = jnp.dot(expert_in, expert_up[0], preferred_element_type=jnp.float32)
    activity = (jax.nn.silu(gate_value) * up_value).astype(jnp.bfloat16)
    expert_share = head_sum_scatter(
        jnp.dot(activity, expert_down[0], preferred_element_type=jnp.float32).astype(jnp.bfloat16),
        1,
    ).astype(jnp.bfloat16)
    returned = lax.all_to_all(
        expert_share.reshape(peer_count, capacity * quarter_width),
        "tok",
        split_axis=0,
        concat_axis=0,
        tiled=True,
    )
    chosen_rows = returned.reshape(slot_total, quarter_width)[route_place]
    expert_mix = jnp.sum(route_weight[:, :, None] * chosen_rows.astype(jnp.float32), axis=1).astype(
        jnp.bfloat16
    )
    return (new_entry, attended, expert_mix)


def solution(mesh):
    in_specs = (
        P("tok", "head"),
        P(),
        P(None, "head"),
        P("head", None),
        P("head", None, None),
        P("head", None, None),
        P("head", None),
        P(("tok", "head"), None),
        P("tok"),
        P("tok"),
        P("head"),
        P("head", None),
        P("tok", None),
        P("tok", None, "head"),
        P("tok", None, "head"),
        P("tok", "head", None),
    )
    out_specs = (P("tok", None), P("tok", "head"), P("tok", "head"))
    return jax.shard_map(body, mesh=mesh, in_specs=in_specs, out_specs=out_specs, check_vma=False)
```

```python
import jax
import jax.numpy as jnp
from jax import lax
from jax.sharding import PartitionSpec as P

D = 2048
NOPE = 128
ROPE = 64
LATENT = 512


NORM_EPS = 1e-06


def rotate_pairs(values, places):
    halfway = values.shape[-1] // 2
    freqs = 10000.0 ** (-jnp.arange(halfway, dtype=jnp.float32) / halfway)
    angles = places.astype(jnp.float32).reshape(places.shape + (1,) * (values.ndim - 1)) * freqs
    cosine = jnp.cos(angles)
    sine = jnp.sin(angles)
    first_half = values[..., :halfway]
    second_half = values[..., halfway:]
    return jnp.concatenate(
        [first_half * cosine - second_half * sine, first_half * sine + second_half * cosine],
        axis=-1,
    )


def owner_attend(all_heads, owner_lengths, latent_cache, head_index, factor):
    slot_rows = all_heads.shape[0]
    total_heads = all_heads.shape[1]
    probe_width = all_heads.shape[2]
    key_rows = latent_cache.shape[0]
    starts = jnp.cumsum(owner_lengths) - owner_lengths
    places = head_index * key_rows + jnp.arange(key_rows, dtype=jnp.int32)
    inside = (places[None, :] >= starts[:, None]) & (
        places[None, :] < (starts + owner_lengths)[:, None]
    )
    scores = factor * jnp.einsum(
        "qc,pc->qp",
        all_heads.reshape(slot_rows * total_heads, probe_width),
        latent_cache,
        preferred_element_type=jnp.float32,
    )
    scores = scores.reshape(slot_rows, total_heads, key_rows)
    weights = jnp.where(inside[:, None, :], jnp.exp(scores), 0.0).astype(jnp.bfloat16)
    numerator = jnp.einsum(
        "khp,pl->khl", weights, latent_cache[:, :LATENT], preferred_element_type=jnp.float32
    )
    denominator = jnp.sum(weights.astype(jnp.float32), axis=2)
    return (numerator, denominator)


def head_sum_scatter(values, axis):
    groups = lax.axis_size("head")
    moved = lax.all_to_all(values, "head", split_axis=axis, concat_axis=0, tiled=True)
    moved = moved.reshape((groups, values.shape[0]) + moved.shape[1:])
    return jnp.sum(moved.astype(jnp.float32), axis=0)


def body(
    hidden,
    attn_gain,
    w_query,
    w_latent,
    w_key_up,
    w_value_up,
    w_out,
    latent_cache,
    cache_lengths,
    request_slot,
    ffn_gain,
    w_router,
    routes,
    expert_gate,
    expert_up,
    expert_down,
):
    local_rows = hidden.shape[0]
    quarter_width = hidden.shape[1]
    local_heads = w_key_up.shape[0]
    peer_count = lax.axis_size("tok")
    head_index = lax.axis_index("head")
    tok_index = lax.axis_index("tok")
    row_ids = jnp.arange(local_rows, dtype=jnp.int32)
    latent_width = w_latent.shape[1]
    head_count = lax.axis_size("head")
    gain_part = lax.dynamic_slice_in_dim(attn_gain, head_index * quarter_width, quarter_width, 0)
    raw_part = jnp.dot(
        (hidden.astype(jnp.float32) * gain_part).astype(jnp.bfloat16),
        w_latent,
        preferred_element_type=jnp.float32,
    )
    part_width = -(-latent_width // 128) * 128
    part_hi = lax.reduce_precision(raw_part, exponent_bits=8, mantissa_bits=7)
    rest = raw_part - part_hi
    part_mid = lax.reduce_precision(rest, exponent_bits=8, mantissa_bits=7)
    part_lo = rest - part_mid
    lane_pad = jnp.zeros((local_rows, part_width - latent_width), jnp.bfloat16)
    send_rows = jnp.concatenate(
        [
            hidden,
            part_hi.astype(jnp.bfloat16),
            lane_pad,
            part_mid.astype(jnp.bfloat16),
            lane_pad,
            part_lo.astype(jnp.bfloat16),
            lane_pad,
        ],
        axis=1,
    )
    got_rows = lax.all_gather(send_rows, "head", axis=0, tiled=False)
    hidden_groups = got_rows[:, :, :quarter_width].astype(jnp.float32)

    def part_piece(k):
        offset = quarter_width + k * part_width
        return got_rows[:, :, offset : offset + latent_width].astype(jnp.float32)

    part_sums = (part_piece(0) + part_piece(1)) + part_piece(2)
    inv_attn = lax.rsqrt(
        jnp.sum(hidden_groups * hidden_groups, axis=(0, 2))[:, None] / D + NORM_EPS
    )
    normed_groups = (
        hidden_groups * inv_attn[None] * attn_gain.reshape(head_count, 1, quarter_width)
    ).astype(jnp.bfloat16)
    compressed = jnp.sum(part_sums, axis=0) * inv_attn
    latent_new = compressed[:, :LATENT]
    latent_new = latent_new * lax.rsqrt(
        jnp.mean(latent_new * latent_new, axis=1, keepdims=True) + NORM_EPS
    )
    new_entry = jnp.concatenate(
        [latent_new, rotate_pairs(compressed[:, LATENT:], cache_lengths)], axis=1
    ).astype(jnp.bfloat16)
    queries = jnp.einsum(
        "gbf,gfq->bq",
        normed_groups,
        w_query.reshape(head_count, quarter_width, w_query.shape[1]),
        preferred_element_type=jnp.float32,
    ).astype(jnp.bfloat16)
    queries = queries.reshape(local_rows, local_heads, NOPE + ROPE)
    absorbed = jnp.einsum(
        "bhn,hnl->bhl", queries[:, :, :NOPE], w_key_up, preferred_element_type=jnp.float32
    ).astype(jnp.bfloat16)
    turned = rotate_pairs(queries[:, :, NOPE:].astype(jnp.float32), cache_lengths).astype(
        jnp.bfloat16
    )
    probes = jnp.concatenate([absorbed, turned], axis=2)
    factor = (NOPE + ROPE) ** (-0.5)
    owner_ids = jnp.arange(peer_count, dtype=jnp.int32)
    dest_owner = request_slot // local_rows
    goes_to = dest_owner[None, :] == owner_ids[:, None]
    sent_any = jnp.max(goes_to.astype(jnp.int32), axis=1)
    sent_row = jnp.sum(jnp.where(goes_to, row_ids[None, :], 0), axis=1)
    sent_slot = request_slot[sent_row]
    sent_len = cache_lengths[sent_row]
    code = jnp.stack(
        [sent_any, sent_slot // 64, sent_slot % 64, sent_len // 64, sent_len % 64], axis=1
    ) * sent_any[:, None]
    code_row = jnp.zeros((peer_count, probes.shape[2]), jnp.float32)
    code_row = code_row.at[:, :5].set(code.astype(jnp.float32)).astype(jnp.bfloat16)
    packed = jnp.concatenate(
        [probes[sent_row], new_entry[sent_row][:, None, :], code_row[:, None, :]], axis=1
    )
    got_packed = lax.all_to_all(packed, "tok", 0, 0, tiled=True)
    got_code = got_packed[:, local_heads + 1, :5].astype(jnp.float32).astype(jnp.int32)
    got_slot = jnp.where(got_code[:, 0] > 0, got_code[:, 1] * 64 + got_code[:, 2], -1)
    got_len = got_code[:, 3] * 64 + got_code[:, 4]
    local_slot = got_slot - tok_index * local_rows
    slot_sel = local_slot[None, :] == row_ids[:, None]
    src_of_slot = jnp.sum(jnp.where(slot_sel, owner_ids[None, :], 0), axis=1)
    owner_probes = got_packed[src_of_slot, :local_heads]
    owner_lengths = got_len[src_of_slot]
    owner_new = got_packed[src_of_slot, local_heads]
    all_heads = lax.all_gather(owner_probes, "head", axis=1, tiled=True)
    numerator, denominator = owner_attend(
        all_heads, owner_lengths, latent_cache, head_index, factor
    )
    den_t = denominator.T
    den_hi = lax.reduce_precision(den_t, exponent_bits=8, mantissa_bits=7)
    den_rest = den_t - den_hi
    den_mid = lax.reduce_precision(den_rest, exponent_bits=8, mantissa_bits=7)
    den_lo = den_rest - den_mid
    den_row = jnp.zeros((3, denominator.shape[1], LATENT), jnp.float32)
    den_row = den_row.at[:, :, : denominator.shape[0]].set(jnp.stack([den_hi, den_mid, den_lo]))
    moved = lax.all_to_all(
        jnp.concatenate([numerator, den_row], axis=0).astype(jnp.bfloat16),
        "head",
        split_axis=1,
        concat_axis=0,
        tiled=True,
    ).astype(jnp.float32)
    moved = moved.reshape((head_count, local_rows + 3) + moved.shape[1:])
    joined = jnp.sum(moved[:, :local_rows], axis=0)
    den_parts = moved[:, local_rows:, :, :local_rows]
    group_den = jnp.sum((den_parts[:, 0] + den_parts[:, 1]) + den_parts[:, 2], axis=0).T
    self_score = factor * jnp.einsum(
        "bhc,bc->bh", owner_probes, owner_new, preferred_element_type=jnp.float32
    )
    self_weight = jnp.exp(self_score).astype(jnp.bfloat16).astype(jnp.float32)
    total_num = joined[:local_rows] + self_weight[:, :, None] * owner_new[:, None, :LATENT].astype(
        jnp.float32
    )
    total_den = group_den + self_weight
    mixed_latent = (total_num / total_den[:, :, None]).astype(jnp.bfloat16)
    owner_out = jnp.einsum(
        "bhl,hld->bhd", mixed_latent, w_value_up, preferred_element_type=jnp.float32
    ).astype(jnp.bfloat16)
    owner_out = owner_out.reshape(local_rows, local_heads * NOPE)
    owner_out = jnp.concatenate(
        [owner_out, jnp.zeros((1, local_heads * NOPE), jnp.bfloat16)], axis=0
    )
    back_valid = (local_slot >= 0) & (local_slot < local_rows)
    back_row = jnp.where(back_valid, local_slot, local_rows)
    head_out = lax.all_to_all(owner_out[back_row], "tok", 0, 0, tiled=True)[dest_owner]
    head_out = head_out.reshape(local_rows, local_heads * NOPE)
    attn_piece = head_sum_scatter(jnp.dot(head_out, w_out, preferred_element_type=jnp.float32), 1)
    attended = (hidden.astype(jnp.float32) + attn_piece).astype(jnp.bfloat16)
    attended_wide = attended.astype(jnp.float32)
    gained = (attended_wide * ffn_gain).astype(jnp.bfloat16)
    squares, logit_part = lax.psum(
        (
            jnp.sum(attended_wide * attended_wide, axis=1),
            jnp.dot(gained, w_router, preferred_element_type=jnp.float32),
        ),
        "head",
    )
    inv_ffn = lax.rsqrt(squares / D + NORM_EPS)
    logits = logit_part * inv_ffn[:, None]
    normed_ffn = (attended_wide * ffn_gain * inv_ffn[:, None]).astype(jnp.bfloat16)
    expert_count = w_router.shape[1]
    route_count = routes.shape[1]
    expert_ids = jnp.arange(expert_count, dtype=jnp.int32)
    named = routes[:, :, None] == expert_ids[None, None, :]
    picked = jnp.sum(jnp.where(named, logits[:, None, :], 0.0), axis=2)
    lifted = jnp.exp(picked)
    route_weight = lifted / jnp.sum(lifted, axis=1, keepdims=True)
    struck = jnp.max(named.astype(jnp.int32), axis=1)
    earlier_hits = jnp.cumsum(struck, axis=0) - struck
    capacity = min(local_rows, max(2, 2 * local_rows * route_count // expert_count))
    route_place = routes * capacity + jnp.take_along_axis(earlier_hits, routes, axis=1)
    slot_total = expert_count * capacity
    slot_ids = jnp.arange(slot_total, dtype=jnp.int32)
    filled = route_place[None, :, :] == slot_ids[:, None, None]
    source_token = jnp.sum(
        jnp.where(filled, row_ids[None, :, None], 0), axis=(1, 2)
    ) + local_rows * (1 - jnp.max(filled.astype(jnp.int32), axis=(1, 2)))
    padded_rows = jnp.concatenate(
        [normed_ffn, jnp.zeros((1, normed_ffn.shape[1]), jnp.bfloat16)], axis=0
    )
    arrived = lax.all_to_all(
        padded_rows[source_token].reshape(expert_count, capacity, quarter_width),
        "tok",
        split_axis=0,
        concat_axis=0,
        tiled=True,
    )
    expert_in = lax.all_to_all(
        jnp.broadcast_to(
            arrived.reshape(1, peer_count * capacity, quarter_width),
            (head_count, peer_count * capacity, quarter_width),
        ),
        "head",
        split_axis=0,
        concat_axis=2,
        tiled=True,
    ).reshape(peer_count * capacity, head_count * quarter_width)
    gate_value = jnp.dot(expert_in, expert_gate[0], preferred_element_type=jnp.float32)
    up_value = jnp.dot(expert_in, expert_up[0], preferred_element_type=jnp.float32)
    activity = (jax.nn.silu(gate_value) * up_value).astype(jnp.bfloat16)
    expert_share = head_sum_scatter(
        jnp.dot(activity, expert_down[0], preferred_element_type=jnp.float32).astype(jnp.bfloat16),
        1,
    ).astype(jnp.bfloat16)
    returned = lax.all_to_all(
        expert_share.reshape(peer_count, capacity, quarter_width),
        "tok",
        split_axis=0,
        concat_axis=0,
        tiled=True,
    )
    chosen_rows = returned.reshape(slot_total, quarter_width)[route_place]
    expert_mix = jnp.sum(route_weight[:, :, None] * chosen_rows.astype(jnp.float32), axis=1).astype(
        jnp.bfloat16
    )
    return (new_entry, attended, expert_mix)


def solution(mesh):
    in_specs = (
        P("tok", "head"),
        P(),
        P(None, "head"),
        P("head", None),
        P("head", None, None),
        P("head", None, None),
        P("head", None),
        P(("tok", "head"), None),
        P("tok"),
        P("tok"),
        P("head"),
        P("head", None),
        P("tok", None),
        P("tok", None, "head"),
        P("tok", None, "head"),
        P("tok", "head", None),
    )
    out_specs = (P("tok", None), P("tok", "head"), P("tok", "head"))
    return jax.shard_map(body, mesh=mesh, in_specs=in_specs, out_specs=out_specs, check_vma=False)
```

```python
import jax
import jax.numpy as jnp
from jax import lax
from jax.sharding import PartitionSpec as P

D = 2048
NOPE = 128
ROPE = 64
LATENT = 512


NORM_EPS = 1e-06


def rotate_pairs(values, places):
    halfway = values.shape[-1] // 2
    freqs = 10000.0 ** (-jnp.arange(halfway, dtype=jnp.float32) / halfway)
    angles = places.astype(jnp.float32).reshape(places.shape + (1,) * (values.ndim - 1)) * freqs
    cosine = jnp.cos(angles)
    sine = jnp.sin(angles)
    first_half = values[..., :halfway]
    second_half = values[..., halfway:]
    return jnp.concatenate(
        [first_half * cosine - second_half * sine, first_half * sine + second_half * cosine],
        axis=-1,
    )


def owner_attend(all_heads, owner_lengths, latent_cache, head_index, factor):
    slot_rows = all_heads.shape[0]
    total_heads = all_heads.shape[1]
    probe_width = all_heads.shape[2]
    key_rows = latent_cache.shape[0]
    starts = jnp.cumsum(owner_lengths) - owner_lengths
    places = head_index * key_rows + jnp.arange(key_rows, dtype=jnp.int32)
    inside = (places[None, :] >= starts[:, None]) & (
        places[None, :] < (starts + owner_lengths)[:, None]
    )
    scores = factor * jnp.einsum(
        "qc,pc->qp",
        all_heads.reshape(slot_rows * total_heads, probe_width),
        latent_cache,
        preferred_element_type=jnp.float32,
    )
    scores = scores.reshape(slot_rows, total_heads, key_rows)
    weights = jnp.where(inside[:, None, :], jnp.exp(scores), 0.0).astype(jnp.bfloat16)
    numerator = jnp.einsum(
        "khp,pl->khl", weights, latent_cache[:, :LATENT], preferred_element_type=jnp.float32
    )
    denominator = jnp.sum(weights.astype(jnp.float32), axis=2)
    return (numerator, denominator)


def head_sum_scatter(values, axis):
    groups = lax.axis_size("head")
    moved = lax.all_to_all(values, "head", split_axis=axis, concat_axis=0, tiled=True)
    moved = moved.reshape((groups, values.shape[0]) + moved.shape[1:])
    return jnp.sum(moved.astype(jnp.float32), axis=0)


def body(
    hidden,
    attn_gain,
    w_query,
    w_latent,
    w_key_up,
    w_value_up,
    w_out,
    latent_cache,
    cache_lengths,
    request_slot,
    ffn_gain,
    w_router,
    routes,
    expert_gate,
    expert_up,
    expert_down,
):
    local_rows = hidden.shape[0]
    quarter_width = hidden.shape[1]
    local_heads = w_key_up.shape[0]
    peer_count = lax.axis_size("tok")
    head_index = lax.axis_index("head")
    tok_index = lax.axis_index("tok")
    row_ids = jnp.arange(local_rows, dtype=jnp.int32)
    latent_width = w_latent.shape[1]
    head_count = lax.axis_size("head")
    gain_part = lax.dynamic_slice_in_dim(attn_gain, head_index * quarter_width, quarter_width, 0)
    raw_part = jnp.dot(
        (hidden.astype(jnp.float32) * gain_part).astype(jnp.bfloat16),
        w_latent,
        preferred_element_type=jnp.float32,
    )
    part_width = -(-latent_width // 128) * 128
    part_hi = lax.reduce_precision(raw_part, exponent_bits=8, mantissa_bits=7)
    rest = raw_part - part_hi
    part_mid = lax.reduce_precision(rest, exponent_bits=8, mantissa_bits=7)
    part_lo = rest - part_mid
    lane_pad = jnp.zeros((local_rows, part_width - latent_width), jnp.bfloat16)
    send_rows = jnp.concatenate(
        [
            hidden,
            part_hi.astype(jnp.bfloat16),
            lane_pad,
            part_mid.astype(jnp.bfloat16),
            lane_pad,
            part_lo.astype(jnp.bfloat16),
            lane_pad,
        ],
        axis=1,
    )
    got_rows = lax.all_gather(send_rows, "head", axis=0, tiled=False)
    hidden_groups = got_rows[:, :, :quarter_width].astype(jnp.float32)

    def part_piece(k):
        offset = quarter_width + k * part_width
        return got_rows[:, :, offset : offset + latent_width].astype(jnp.float32)

    part_sums = (part_piece(0) + part_piece(1)) + part_piece(2)
    inv_attn = lax.rsqrt(
        jnp.sum(hidden_groups * hidden_groups, axis=(0, 2))[:, None] / D + NORM_EPS
    )
    normed_groups = (
        hidden_groups * inv_attn[None] * attn_gain.reshape(head_count, 1, quarter_width)
    ).astype(jnp.bfloat16)
    compressed = jnp.sum(part_sums, axis=0) * inv_attn
    latent_new = compressed[:, :LATENT]
    latent_new = latent_new * lax.rsqrt(
        jnp.mean(latent_new * latent_new, axis=1, keepdims=True) + NORM_EPS
    )
    new_entry = jnp.concatenate(
        [latent_new, rotate_pairs(compressed[:, LATENT:], cache_lengths)], axis=1
    ).astype(jnp.bfloat16)
    queries = jnp.einsum(
        "gbf,gfq->bq",
        normed_groups,
        w_query.reshape(head_count, quarter_width, w_query.shape[1]),
        preferred_element_type=jnp.float32,
    ).astype(jnp.bfloat16)
    queries = queries.reshape(local_rows, local_heads, NOPE + ROPE)
    absorbed = jnp.einsum(
        "bhn,hnl->bhl", queries[:, :, :NOPE], w_key_up, preferred_element_type=jnp.float32
    ).astype(jnp.bfloat16)
    turned = rotate_pairs(queries[:, :, NOPE:].astype(jnp.float32), cache_lengths).astype(
        jnp.bfloat16
    )
    probes = jnp.concatenate([absorbed, turned], axis=2)
    factor = (NOPE + ROPE) ** (-0.5)
    owner_ids = jnp.arange(peer_count, dtype=jnp.int32)
    dest_owner = request_slot // local_rows
    goes_to = dest_owner[None, :] == owner_ids[:, None]
    sent_any = jnp.max(goes_to.astype(jnp.int32), axis=1)
    sent_row = jnp.sum(jnp.where(goes_to, row_ids[None, :], 0), axis=1)
    sent_slot = request_slot[sent_row]
    sent_len = cache_lengths[sent_row]
    code = jnp.stack(
        [sent_any, sent_slot // 64, sent_slot % 64, sent_len // 64, sent_len % 64], axis=1
    ) * sent_any[:, None]
    code_row = jnp.zeros((peer_count, probes.shape[2]), jnp.float32)
    code_row = code_row.at[:, :5].set(code.astype(jnp.float32)).astype(jnp.bfloat16)
    packed = jnp.concatenate(
        [probes[sent_row], new_entry[sent_row][:, None, :], code_row[:, None, :]], axis=1
    )
    got_packed = lax.all_to_all(packed, "tok", 0, 0, tiled=True)
    got_code = got_packed[:, local_heads + 1, :5].astype(jnp.float32).astype(jnp.int32)
    got_slot = jnp.where(got_code[:, 0] > 0, got_code[:, 1] * 64 + got_code[:, 2], -1)
    got_len = got_code[:, 3] * 64 + got_code[:, 4]
    local_slot = got_slot - tok_index * local_rows
    slot_sel = local_slot[None, :] == row_ids[:, None]
    src_of_slot = jnp.sum(jnp.where(slot_sel, owner_ids[None, :], 0), axis=1)
    owner_probes = got_packed[src_of_slot, :local_heads]
    owner_lengths = got_len[src_of_slot]
    owner_new = got_packed[src_of_slot, local_heads]
    all_heads = lax.all_gather(owner_probes, "head", axis=1, tiled=True)
    numerator, denominator = owner_attend(
        all_heads, owner_lengths, latent_cache, head_index, factor
    )
    den_t = denominator.T
    den_hi = lax.reduce_precision(den_t, exponent_bits=8, mantissa_bits=7)
    den_rest = den_t - den_hi
    den_mid = lax.reduce_precision(den_rest, exponent_bits=8, mantissa_bits=7)
    den_lo = den_rest - den_mid
    den_row = jnp.zeros((3, denominator.shape[1], LATENT), jnp.float32)
    den_row = den_row.at[:, :, : denominator.shape[0]].set(jnp.stack([den_hi, den_mid, den_lo]))
    moved = lax.all_to_all(
        jnp.concatenate([numerator, den_row], axis=0).astype(jnp.bfloat16),
        "head",
        split_axis=1,
        concat_axis=0,
        tiled=True,
    ).astype(jnp.float32)
    moved = moved.reshape((head_count, local_rows + 3) + moved.shape[1:])
    joined = jnp.sum(moved[:, :local_rows], axis=0)
    den_parts = moved[:, local_rows:, :, :local_rows]
    group_den = jnp.sum((den_parts[:, 0] + den_parts[:, 1]) + den_parts[:, 2], axis=0).T
    self_score = factor * jnp.einsum(
        "bhc,bc->bh", owner_probes, owner_new, preferred_element_type=jnp.float32
    )
    self_weight = jnp.exp(self_score).astype(jnp.bfloat16).astype(jnp.float32)
    total_num = joined[:local_rows] + self_weight[:, :, None] * owner_new[:, None, :LATENT].astype(
        jnp.float32
    )
    total_den = group_den + self_weight
    mixed_latent = (total_num / total_den[:, :, None]).astype(jnp.bfloat16)
    owner_out = jnp.einsum(
        "bhl,hld->bhd", mixed_latent, w_value_up, preferred_element_type=jnp.float32
    ).astype(jnp.bfloat16)
    owner_out = owner_out.reshape(local_rows, local_heads * NOPE)
    owner_out = jnp.concatenate(
        [owner_out, jnp.zeros((1, local_heads * NOPE), jnp.bfloat16)], axis=0
    )
    back_valid = (local_slot >= 0) & (local_slot < local_rows)
    back_row = jnp.where(back_valid, local_slot, local_rows)
    head_out = lax.all_to_all(owner_out[back_row], "tok", 0, 0, tiled=True)[dest_owner]
    head_out = head_out.reshape(local_rows, local_heads * NOPE)
    attn_piece = head_sum_scatter(
        jnp.dot(head_out, w_out, preferred_element_type=jnp.float32).astype(jnp.bfloat16), 1
    )
    attended = (hidden.astype(jnp.float32) + attn_piece).astype(jnp.bfloat16)
    attended_wide = attended.astype(jnp.float32)
    gained = (attended_wide * ffn_gain).astype(jnp.bfloat16)
    squares, logit_part = lax.psum(
        (
            jnp.sum(attended_wide * attended_wide, axis=1),
            jnp.dot(gained, w_router, preferred_element_type=jnp.float32),
        ),
        "head",
    )
    inv_ffn = lax.rsqrt(squares / D + NORM_EPS)
    logits = logit_part * inv_ffn[:, None]
    normed_ffn = (attended_wide * ffn_gain * inv_ffn[:, None]).astype(jnp.bfloat16)
    expert_count = w_router.shape[1]
    route_count = routes.shape[1]
    expert_ids = jnp.arange(expert_count, dtype=jnp.int32)
    named = routes[:, :, None] == expert_ids[None, None, :]
    picked = jnp.sum(jnp.where(named, logits[:, None, :], 0.0), axis=2)
    lifted = jnp.exp(picked)
    route_weight = lifted / jnp.sum(lifted, axis=1, keepdims=True)
    struck = jnp.max(named.astype(jnp.int32), axis=1)
    earlier_hits = jnp.cumsum(struck, axis=0) - struck
    capacity = min(local_rows, max(2, 2 * local_rows * route_count // expert_count))
    route_place = routes * capacity + jnp.take_along_axis(earlier_hits, routes, axis=1)
    slot_total = expert_count * capacity
    slot_ids = jnp.arange(slot_total, dtype=jnp.int32)
    filled = route_place[None, :, :] == slot_ids[:, None, None]
    source_token = jnp.sum(
        jnp.where(filled, row_ids[None, :, None], 0), axis=(1, 2)
    ) + local_rows * (1 - jnp.max(filled.astype(jnp.int32), axis=(1, 2)))
    padded_rows = jnp.concatenate(
        [normed_ffn, jnp.zeros((1, normed_ffn.shape[1]), jnp.bfloat16)], axis=0
    )
    arrived = lax.all_to_all(
        padded_rows[source_token].reshape(expert_count, capacity, quarter_width),
        "tok",
        split_axis=0,
        concat_axis=0,
        tiled=True,
    )
    expert_in = lax.all_to_all(
        jnp.broadcast_to(
            arrived.reshape(1, peer_count * capacity, quarter_width),
            (head_count, peer_count * capacity, quarter_width),
        ),
        "head",
        split_axis=0,
        concat_axis=2,
        tiled=True,
    ).reshape(peer_count * capacity, head_count * quarter_width)
    gate_value = jnp.dot(expert_in, expert_gate[0], preferred_element_type=jnp.float32)
    up_value = jnp.dot(expert_in, expert_up[0], preferred_element_type=jnp.float32)
    activity = (jax.nn.silu(gate_value) * up_value).astype(jnp.bfloat16)
    expert_share = head_sum_scatter(
        jnp.dot(activity, expert_down[0], preferred_element_type=jnp.float32).astype(jnp.bfloat16),
        1,
    ).astype(jnp.bfloat16)
    returned = lax.all_to_all(
        expert_share.reshape(peer_count, capacity, quarter_width),
        "tok",
        split_axis=0,
        concat_axis=0,
        tiled=True,
    )
    chosen_rows = returned.reshape(slot_total, quarter_width)[route_place]
    expert_mix = jnp.sum(route_weight[:, :, None] * chosen_rows.astype(jnp.float32), axis=1).astype(
        jnp.bfloat16
    )
    return (new_entry, attended, expert_mix)


def solution(mesh):
    in_specs = (
        P("tok", "head"),
        P(),
        P(None, "head"),
        P("head", None),
        P("head", None, None),
        P("head", None, None),
        P("head", None),
        P(("tok", "head"), None),
        P("tok"),
        P("tok"),
        P("head"),
        P("head", None),
        P("tok", None),
        P("tok", None, "head"),
        P("tok", None, "head"),
        P("tok", "head", None),
    )
    out_specs = (P("tok", None), P("tok", "head"), P("tok", "head"))
    return jax.shard_map(body, mesh=mesh, in_specs=in_specs, out_specs=out_specs, check_vma=False)
```
